512 devices in a mesh: dp: 8 (over x, core), expert: 64 (over y, z).
Axes of the slice: x: 4, y: 4, z: 16, core: 2. Of those that a mesh axis runs over, the one named last changes fastest.
Arguments:
- query_rows: bfloat16 [65536, 2048], P(('dp', 'expert')), may hold values from -40 to 40
- key_rows: bfloat16 [65536, 256], P(('dp', 'expert')), may hold values from -40 to 40
- value_rows: bfloat16 [65536, 256], P(('dp', 'expert')), may hold values from -6 to 6
- residual: bfloat16 [65536, 1024], P(('dp', 'expert')), may hold values from -25 to 25
- document_owner: int32 [512, 8], P(('dp', 'expert')), may hold values from 0 to 7, as said below
- document_length: int32 [512, 8], P(('dp', 'expert')), may hold values from 8 to 24, as said below
- document_offset: int32 [512, 8], P(('dp', 'expert')), may hold values from 0 to 120, as said below
- query_gain: float32 [128], replicated, may hold values from 0.3 to 5.5
- key_gain: float32 [128], replicated, may hold values from 0.3 to 5.5
- output_weight: bfloat16 [2048, 1024], P('expert'), may hold values from -0.125 to 0.125
- post_gain: float32 [1024], replicated, may hold values from 0.5 to 2
- routes: int32 [65536, 8], P(('dp', 'expert')), may hold values from 0 to 63, all different within a row; in each aligned block of 128 rows (0 to 127, 128 to 255, ...) at most 20 rows name the same one
- route_weight: float32 [65536, 8], P(('dp', 'expert')), may hold values from 0.1 to 1
- gate_weight: bfloat16 [64, 768, 1024], P('expert', 'dp'), may hold values from -0.1875 to 0.1875
- up_weight: bfloat16 [64, 768, 1024], P('expert', 'dp'), may hold values from -0.1875 to 0.1875
- down_weight: bfloat16 [64, 768, 1024], P('expert', 'dp'), may hold values from -0.21875 to 0.21875
Outputs:
- layer_out: bfloat16 [65536, 1024], P(('dp', 'expert'))
The draws below stay inside these ranges and needn't reach their ends.
Inputs may be any that keep to these rules, and one draw needn't show every extreme that they name: `document_owner`: each device's row names every dp index once, so a device sends exactly one document to each pack owner of its expert column. `document_length`: A device's lengths sum to 128; the documents that all devices of an expert column send to one owner also sum to 128; no device sends more than 24 rows to one owner, and some device does in every column. `document_offset`: the documents that reach one owner cover its 128 pack rows exactly once. `routes`: at most 20 of one device's rows name one expert; a row names 8 different experts.
All inputs are finite; a program needn't handle non-finite values.
Results may differ from the reference program's by a relative error of at most 0.012.
The reference program's roundings to bfloat16 on the way count: a program that leaves them out, or rounds other values in their place, can miss the bound.
Values may be sent and summed in bfloat16 or wider, within the bound.
No kernel may reach another device: no remote copies, remote signals or barrier semaphores. Data moves between devices by JAX's collectives and lax.ppermute only.
A program may use at most 64 MiB of HBM per device.

```python
import math
import jax
import jax.numpy as jnp
import numpy as np
from jax import lax

D = 1024
HEADS = 16
KV_HEADS = 2
HEAD_DIM = 128
MOE_FF = 768
TOP = 8
TOK_DEV = 128
TOKENS = 65536
EXPERTS = 64
DOC_CAP = 24
MOST = 20
N_DP = 8
N_EXPERT = 64


def one_permutation(subkey):
    return jax.random.permutation(subkey, N_DP)


def document_tables(key):
    base_rows = TOK_DEV // N_DP
    reach = DOC_CAP - base_rows
    seeds = jax.random.split(jax.random.fold_in(key, 404), 5)
    levels = jax.random.randint(seeds[0], (N_EXPERT, N_DP), 0, reach + 1)
    pivot = jax.random.randint(seeds[1], (N_EXPERT, 1), 0, N_DP)
    owner_ids = jnp.arange(N_DP, dtype=jnp.int32)[None, :]
    levels = jnp.where(owner_ids == (pivot + 2) % N_DP, reach, levels)
    levels = jnp.where(owner_ids == (pivot + 1) % N_DP, 0, levels)
    levels = jnp.where(owner_ids == pivot, reach, levels)
    shifts = levels - jnp.roll(levels, -1, axis=1)
    spread = jax.vmap(one_permutation)(jax.random.split(seeds[2], N_EXPERT))
    source_ids = jnp.arange(N_DP, dtype=jnp.int32)
    diagonal = (spread[:, None, :] - source_ids[None, :, None]) % N_DP
    picked = diagonal[..., None] == source_ids[None, None, None, :]
    counts = base_rows + jnp.sum(jnp.where(picked, shifts[:, None, None, :], 0), axis=3)
    order = jax.vmap(one_permutation)(jax.random.split(seeds[3], N_EXPERT * N_DP)).reshape(N_EXPERT, N_DP, N_DP)
    places = jax.vmap(one_permutation)(jax.random.split(seeds[4], N_EXPERT * N_DP)).reshape(N_EXPERT, N_DP, N_DP)
    counts_by_owner = jnp.transpose(counts, (0, 2, 1))
    ahead = places[:, :, None, :] < places[:, :, :, None]
    offsets_by_owner = jnp.sum(jnp.where(ahead, counts_by_owner[:, :, None, :], 0), axis=3)
    offsets = jnp.transpose(offsets_by_owner, (0, 2, 1))
    select = order[..., None] == source_ids[None, None, None, :]
    lengths = jnp.sum(jnp.where(select, counts[:, :, None, :], 0), axis=3)
    starts_in_pack = jnp.sum(jnp.where(select, offsets[:, :, None, :], 0), axis=3)

    def arrange(table):
        return jnp.transpose(table, (1, 0, 2)).reshape(N_DP * N_EXPERT, N_DP).astype(jnp.int32)
    return (arrange(order), arrange(lengths), arrange(starts_in_pack))


def draw_document_owner(key, part):
    return document_tables(key)[0]


def draw_document_length(key, part):
    return document_tables(key)[1]


def draw_document_offset(key, part):
    return document_tables(key)[2]


def query_key_pair(key):
    seeds = jax.random.split(jax.random.fold_in(key, 505), 4)
    key_scale = jnp.exp(jax.random.uniform(seeds[0], (1, KV_HEADS, HEAD_DIM), minval=0.0, maxval=math.log(10.0)))
    query_scale = jnp.exp(jax.random.uniform(seeds[1], (1, HEADS, HEAD_DIM), minval=0.0, maxval=math.log(10.0)))
    key_noise = jnp.clip(jax.random.normal(seeds[2], (TOKENS, KV_HEADS, HEAD_DIM)), -4.0, 4.0)
    query_noise = jnp.clip(jax.random.normal(seeds[3], (TOKENS, HEADS, HEAD_DIM)), -4.0, 4.0)
    keys_out = key_noise * key_scale
    queries_out = query_noise * query_scale
    queries_flat = queries_out.reshape(TOKENS, HEADS * HEAD_DIM).astype(jnp.bfloat16)
    keys_flat = keys_out.reshape(TOKENS, KV_HEADS * HEAD_DIM).astype(jnp.bfloat16)
    return (queries_flat, keys_flat)


def draw_query_rows(key, part):
    return query_key_pair(key)[0]


def draw_key_rows(key, part):
    return query_key_pair(key)[1]


def gain_values(key, salt):
    subkey = jax.random.fold_in(key, salt)
    return jax.random.uniform(subkey, (HEAD_DIM,), minval=0.3, maxval=1.0).astype(jnp.float32)


def draw_query_gain(key, part):
    return gain_values(key, 606)


def draw_key_gain(key, part):
    return gain_values(key, 707)


def draw_residual(key, part):
    seeds = jax.random.split(jax.random.fold_in(key, 808), 3)
    rows_scale = jnp.exp(jax.random.uniform(seeds[0], (TOKENS, 1), minval=math.log(0.25), maxval=math.log(2.5)))
    columns_scale = jnp.exp(jax.random.uniform(seeds[1], (1, D), minval=math.log(0.25), maxval=math.log(2.5)))
    noise = jnp.clip(jax.random.normal(seeds[2], (TOKENS, D)), -4.0, 4.0)
    return (noise * rows_scale * columns_scale).astype(jnp.bfloat16)


def shard_levels(key, dims, cuts, smallest, high):
    loudness, own = 1.0, jax.random.fold_in(key, 6)
    for dim, parts in cuts:
        draws = jnp.exp(jax.random.uniform(jax.random.fold_in(own, dim), (parts,), jnp.float32, smallest / len(cuts), high / len(cuts)))
        loudness = loudness * jnp.repeat(draws, dims[dim] // parts).reshape([-1 if axis == dim else 1 for axis in range(len(dims))])
    return loudness


def shared_out(key, own, number, rows, count, top, most, slope):
    order = jax.random.permutation(key, count)
    packed, common = load_shares(count, rows * top, most, slope, True), load_shares(count, rows * top, most, slope, False)
    places = jnp.arange(count)

    def named(sizes, turn):
        used = int((sizes > 0).sum())
        fixed = max(1, used // 4)
        passed = fixed + (places - fixed + turn * (used - fixed)) % max(1, count - fixed)
        return jnp.zeros((count,), jnp.int32).at[order[jnp.where(places < fixed, places, passed)]].set(jnp.asarray(sizes, jnp.int32))

    sizes = jnp.where(number % 4 == 0, named(packed, number // 4), named(common, number - number // 4 - 1))
    mixed = jax.random.permutation(jax.random.fold_in(own, 3), count)
    giver, sink = mixed[0:count // 2 * 2:2], mixed[1:count // 2 * 2:2]
    room = jnp.minimum(sizes[giver] - 1, most - sizes[sink]) // 2
    room = jnp.where((giver == order[0]) | (sink == order[0]) | (sizes[sink] == 0), 0, jnp.maximum(room, 0))
    passed = jax.random.randint(jax.random.fold_in(own, 4), (count // 2,), 0, 1 << 20) % (room + 1)
    sizes = sizes.at[giver].add(-passed).at[sink].add(passed)
    members = jnp.searchsorted(jnp.cumsum(sizes), jnp.arange(rows * top), side="right").astype(jnp.int32)
    table = members.reshape(top, rows).T
    table = table[jax.random.permutation(jax.random.fold_in(own, 1), rows)]
    turn = jax.random.randint(jax.random.fold_in(own, 2), (rows, 1), 0, top)
    return jnp.take_along_axis(table, (jnp.arange(top)[None, :] + turn) % top, axis=1)


def load_shares(number_of, total, bound, skew, full):
    weights = [(1 << 20) // math.isqrt(standing ** skew) + 1 for standing in range(1, number_of + 1)]
    largest = bound if full else min(bound, max(-(-total // number_of), total * weights[0] // sum(weights)))
    least = 1 if total - largest >= number_of - 1 else 0
    given, surplus = [largest] + [least] * (number_of - 1), total - largest - least * (number_of - 1)
    while surplus > 0:
        candidates = [i for i in range(1, number_of) if given[i] < largest] or [i for i in range(1, number_of) if given[i] < bound]
        whole, left = sum([weights[i] for i in candidates]), surplus
        for i in candidates:
            more = min(bound - given[i], max(1, left * weights[i] // whole), surplus)
            given[i] = given[i] + more
            surplus = surplus - more
    return np.array(given)


def centred(own_key, extent, scale, most, shards=(), kind=jnp.bfloat16):
    entries = scale * jax.random.normal(own_key, extent, jnp.float32)
    if shards:
        entries = entries * shard_levels(own_key, extent, shards, -0.22, 0.18)
    return jnp.clip(entries, -most, most).astype(kind)


def setup_inputs(seed: int = 0) -> dict:
    keys = jax.random.split(jax.random.key(seed), 17)
    query_rows = draw_query_rows(jax.random.fold_in(keys[16], 71), 0)
    key_rows = draw_key_rows(jax.random.fold_in(keys[16], 71), 0)
    value_rows = centred(keys[2], (TOKENS, KV_HEADS * HEAD_DIM), 1.0, 6.0, ((0, 512),))
    residual = draw_residual(jax.random.fold_in(keys[16], 71), 0)
    document_owner = draw_document_owner(jax.random.fold_in(keys[16], 71), 0)
    document_length = draw_document_length(jax.random.fold_in(keys[16], 71), 0)
    document_offset = draw_document_offset(jax.random.fold_in(keys[16], 71), 0)
    query_gain = draw_query_gain(jax.random.fold_in(keys[16], 71), 0)
    key_gain = draw_key_gain(jax.random.fold_in(keys[16], 71), 0)
    output_weight = centred(keys[9], (HEADS * HEAD_DIM, D), (HEADS * HEAD_DIM) ** -0.5, 0.125, ((0, 64),))
    post_gain = jnp.clip(jnp.exp(jax.random.uniform(keys[10], (D,), jnp.float32, math.log(0.5), math.log(2.0))), 0.5, 2.0)
    routes_keys = jax.random.split(jax.random.fold_in(keys[11], 1), TOKENS // TOK_DEV)
    routes_turns = jax.random.permutation(jax.random.fold_in(keys[11], 3), TOKENS // TOK_DEV)
    routes = jax.vmap(lambda own, number: shared_out(jax.random.fold_in(keys[11], 2), own, number, TOK_DEV, EXPERTS, TOP, MOST, 1))(routes_keys, routes_turns).reshape((TOKENS, TOP))
    route_weight = jnp.clip(jnp.exp(math.log(1.0) - 2.3025851 * jax.random.uniform(keys[12], (TOKENS, TOP), jnp.float32) ** shard_levels(keys[12], (TOKENS, TOP), ((0, 512),), -0.2, 0.2)), 0.1, 1.0)
    gate_weight = centred(keys[13], (EXPERTS, MOE_FF, D), D ** -0.5, 0.1875, ((0, 64), (1, 8)))
    up_weight = centred(keys[14], (EXPERTS, MOE_FF, D), D ** -0.5, 0.1875, ((0, 64), (1, 8)))
    down_weight = centred(keys[15], (EXPERTS, MOE_FF, D), MOE_FF ** -0.5, 0.21875, ((0, 64), (1, 8)))
    return {"query_rows": query_rows, "key_rows": key_rows, "value_rows": value_rows, "residual": residual, "document_owner": document_owner, "document_length": document_length, "document_offset": document_offset, "query_gain": query_gain, "key_gain": key_gain, "output_weight": output_weight, "post_gain": post_gain, "routes": routes, "route_weight": route_weight, "gate_weight": gate_weight, "up_weight": up_weight, "down_weight": down_weight}


norm_epsilon = 1e-06
rope_base = 1000000.0

def rms_scale(values, gain):
    mean_square = lax.optimization_barrier(jnp.mean(values * values, axis=-1, keepdims=True))
    return values * lax.rsqrt(mean_square + norm_epsilon) * gain

def rotary(values, positions):
    head_width = values.shape[-1]
    half_width = head_width // 2
    frequency = rope_base ** (-2.0 * jnp.arange(half_width, dtype=jnp.float32) / head_width)
    angles = positions.astype(jnp.float32)[:, None] * frequency[None, :]
    cosine_part = jnp.cos(angles)[:, None, :]
    sine_part = jnp.sin(angles)[:, None, :]
    leading = values[..., :half_width]
    trailing = values[..., half_width:]
    return jnp.concatenate([leading * cosine_part - trailing * sine_part, trailing * cosine_part + leading * sine_part], axis=-1)

def pack_layout(document_owner, document_length, document_offset):
    device_total = N_DP * N_EXPERT
    starts = jnp.cumsum(document_length, axis=1) - document_length
    ends = starts + document_length
    row_ids = jnp.arange(TOK_DEV, dtype=jnp.int32)
    inside = (row_ids[None, :, None] >= starts[:, None, :]) & (row_ids[None, :, None] < ends[:, None, :])
    doc_ids = jnp.arange(N_DP, dtype=jnp.int32)
    which_doc = lax.optimization_barrier(jnp.sum(jnp.where(inside, doc_ids[None, None, :], 0), axis=2)).astype(jnp.int32)
    owner_of = lax.optimization_barrier(jnp.sum(jnp.where(inside, document_owner[:, None, :], 0), axis=2)).astype(jnp.int32)
    start_of = lax.optimization_barrier(jnp.sum(jnp.where(inside, starts[:, None, :], 0), axis=2)).astype(jnp.int32)
    offset_of = lax.optimization_barrier(jnp.sum(jnp.where(inside, document_offset[:, None, :], 0), axis=2)).astype(jnp.int32)
    within = row_ids[None, :] - start_of
    column = (jnp.arange(device_total, dtype=jnp.int32) % N_EXPERT)[:, None]
    target = (owner_of * N_EXPERT + column) * TOK_DEV + offset_of + within
    identity = jnp.arange(device_total, dtype=jnp.int32)[:, None] * N_DP + which_doc
    return (target.reshape(-1), identity.reshape(-1), within.reshape(-1))

def attend(query_part, key_part, value_part, identity, position, query_gain, key_gain):
    row_total = query_part.shape[0]
    group_size = HEADS // KV_HEADS
    queries = rotary(rms_scale(query_part.reshape(row_total, HEADS, HEAD_DIM).astype(jnp.float32), query_gain), position).astype(jnp.bfloat16)
    keys_normed = rotary(rms_scale(key_part.reshape(row_total, KV_HEADS, HEAD_DIM).astype(jnp.float32), key_gain), position).astype(jnp.bfloat16)
    queries = queries.reshape(row_total, KV_HEADS, group_size, HEAD_DIM).astype(jnp.float32)
    scores = jnp.einsum('pkgd,qkd->kgpq', queries, keys_normed.astype(jnp.float32)) * HEAD_DIM ** (-0.5)
    allowed = (identity[:, None] == identity[None, :]) & (position[None, :] <= position[:, None])
    scores = jnp.where(allowed, scores, -jnp.inf)
    largest = lax.optimization_barrier(jnp.max(scores, axis=-1, keepdims=True))
    powers = jnp.exp(scores - largest)
    weights = (powers / lax.optimization_barrier(jnp.sum(powers, axis=-1, keepdims=True))).astype(jnp.bfloat16)
    values_heads = value_part.reshape(row_total, KV_HEADS, HEAD_DIM).astype(jnp.float32)
    mixed = jnp.einsum('kgpq,qkd->pkgd', weights.astype(jnp.float32), values_heads)
    return mixed.astype(jnp.bfloat16).reshape(row_total, HEADS * HEAD_DIM)

def reference(query_rows, key_rows, value_rows, residual, document_owner, document_length, document_offset, query_gain, key_gain, output_weight, post_gain, routes, route_weight, gate_weight, up_weight, down_weight):
    device_total = N_DP * N_EXPERT
    target, identity, within = pack_layout(document_owner, document_length, document_offset)
    pack_query = jnp.zeros_like(query_rows).at[target].set(query_rows)
    pack_key = jnp.zeros_like(key_rows).at[target].set(key_rows)
    pack_value = jnp.zeros_like(value_rows).at[target].set(value_rows)
    pack_residual = jnp.zeros_like(residual).at[target].set(residual)
    pack_identity = jnp.zeros_like(identity).at[target].set(identity)
    pack_position = jnp.zeros_like(within).at[target].set(within)

    def attend_pack(pieces):
        return attend(pieces[0], pieces[1], pieces[2], pieces[3], pieces[4], query_gain, key_gain)
    attended = lax.map(attend_pack, (pack_query.reshape(device_total, TOK_DEV, -1), pack_key.reshape(device_total, TOK_DEV, -1), pack_value.reshape(device_total, TOK_DEV, -1), pack_identity.reshape(device_total, TOK_DEV), pack_position.reshape(device_total, TOK_DEV)))
    attended = attended.reshape(TOKENS, HEADS * HEAD_DIM)
    hidden_state = pack_residual.astype(jnp.float32) + jnp.dot(attended, output_weight, preferred_element_type=jnp.float32)
    normed = rms_scale(hidden_state, post_gain).astype(jnp.bfloat16)
    expert_ids = jnp.arange(EXPERTS, dtype=jnp.int32)
    chosen = lax.optimization_barrier(jnp.sum((routes[:, :, None] == expert_ids[None, None, :]).astype(jnp.int32), axis=1))
    per_device = chosen.reshape(device_total, TOK_DEV, EXPERTS)
    rank = (jnp.cumsum(per_device, axis=1) - per_device).reshape(TOKENS, EXPERTS).astype(jnp.int32)
    copy_rank = jnp.take_along_axis(rank, routes, axis=1).astype(jnp.int32)
    owner_device = jnp.arange(TOKENS, dtype=jnp.int32) // TOK_DEV
    slot = owner_device[:, None] * MOST + copy_rank
    token_ids = jnp.broadcast_to(jnp.arange(TOKENS, dtype=jnp.int32)[:, None], routes.shape)
    gates = route_weight / lax.optimization_barrier(jnp.sum(route_weight, axis=1, keepdims=True))
    table = jnp.zeros((EXPERTS, device_total * MOST), jnp.int32).at[routes, slot].set(token_ids)
    weight_table = jnp.zeros((EXPERTS, device_total * MOST), jnp.float32).at[routes, slot].set(gates)

    def one_expert(total, pieces):
        gate_part, up_part, down_part, index_row, weight_row = pieces
        rows = normed[index_row]
        gate_value = jnp.dot(rows, gate_part.T, preferred_element_type=jnp.float32)
        up_value = jnp.dot(rows, up_part.T, preferred_element_type=jnp.float32)
        active = (jax.nn.silu(gate_value) * up_value).astype(jnp.bfloat16)
        produced = jnp.dot(active, down_part, preferred_element_type=jnp.float32).astype(jnp.bfloat16)
        return (total.at[index_row].add(weight_row[:, None] * produced.astype(jnp.float32)), None)
    mixture, unused = lax.scan(one_expert, jnp.zeros((TOKENS, D), jnp.float32), (gate_weight, up_weight, down_weight, table, weight_table))
    return (hidden_state + mixture).astype(jnp.bfloat16)
```

```python
import jax
import jax.numpy as jnp
from jax import lax
from jax.sharding import PartitionSpec as P

norm_epsilon = 1e-06
rope_base = 1000000.0


def rms_scale(values, gain):
    mean_square = jnp.mean(values * values, axis=-1, keepdims=True)
    return values * lax.rsqrt(mean_square + norm_epsilon) * gain


def rotary(values, positions):
    head_width = values.shape[-1]
    half_width = head_width // 2
    frequency = rope_base ** (-2.0 * jnp.arange(half_width, dtype=jnp.float32) / head_width)
    angles = positions.astype(jnp.float32)[:, None] * frequency[None, :]
    cosine_part = jnp.cos(angles)[:, None, :]
    sine_part = jnp.sin(angles)[:, None, :]
    leading = values[..., :half_width]
    trailing = values[..., half_width:]
    return jnp.concatenate(
        [
            leading * cosine_part - trailing * sine_part,
            trailing * cosine_part + leading * sine_part,
        ],
        axis=-1,
    )


def attend(query_part, key_part, value_part, identity, position, query_gain, key_gain):
    row_total = query_part.shape[0]
    head_width = query_gain.shape[0]
    head_count = query_part.shape[1] // head_width
    key_heads = key_part.shape[1] // head_width
    group_size = head_count // key_heads
    queries = rotary(
        rms_scale(
            query_part.reshape(row_total, head_count, head_width).astype(jnp.float32), query_gain
        ),
        position,
    ).astype(jnp.bfloat16)
    keys_normed = rotary(
        rms_scale(key_part.reshape(row_total, key_heads, head_width).astype(jnp.float32), key_gain),
        position,
    ).astype(jnp.bfloat16)
    queries = queries.reshape(row_total, key_heads, group_size, head_width)
    scores = jnp.einsum(
        "pkgd,qkd->kgpq", queries, keys_normed, preferred_element_type=jnp.float32
    ) * head_width ** (-0.5)
    allowed = (identity[:, None] == identity[None, :]) & (position[None, :] <= position[:, None])
    scores = jnp.where(allowed, scores, -jnp.inf)
    largest = jnp.max(scores, axis=-1, keepdims=True)
    powers = jnp.exp(scores - largest)
    weights = (powers / jnp.sum(powers, axis=-1, keepdims=True)).astype(jnp.bfloat16)
    values_heads = value_part.reshape(row_total, key_heads, head_width)
    mixed = jnp.einsum("kgpq,qkd->pkgd", weights, values_heads, preferred_element_type=jnp.float32)
    return mixed.astype(jnp.bfloat16).reshape(row_total, head_count * head_width)


def ring_pairs(rows, cols, step_row, step_col):
    return [
        (r * cols + c, ((r + step_row) % rows) * cols + (c + step_col) % cols)
        for r in range(rows)
        for c in range(cols)
    ]


def ring_gather(block, rows, cols):
    up = lax.ppermute(block, "expert", ring_pairs(rows, cols, 1, 0))
    down = lax.ppermute(block, "expert", ring_pairs(rows, cols, -1, 0))
    up_two = lax.ppermute(up, "expert", ring_pairs(rows, cols, 1, 0))
    by_row = jnp.stack([block, down, up_two, up])
    relative = {0: by_row}
    right = by_row
    left = by_row
    half = cols // 2
    for step in range(1, half + 1):
        right = lax.ppermute(right, "expert", ring_pairs(rows, cols, 0, 1))
        relative[-step % cols] = right
        if step < half:
            left = lax.ppermute(left, "expert", ring_pairs(rows, cols, 0, -1))
            relative[step] = left
    return jnp.stack([relative[k] for k in range(cols)], axis=1)


def project_heads(attended, output_weight):
    expert_total = lax.axis_size("expert")
    cols = 16
    rows = expert_total // cols
    if rows != 4 or expert_total % cols:
        return jnp.dot(
            attended,
            lax.all_gather(output_weight, "expert", axis=0, tiled=True),
            preferred_element_type=jnp.float32,
        )
    own = lax.axis_index("expert")
    own_row = own // cols
    own_col = own % cols
    gathered = ring_gather(output_weight, rows, cols)
    block = output_weight.shape[0]
    row_order = (own_row + jnp.arange(rows, dtype=jnp.int32)) % rows
    col_order = (own_col + jnp.arange(cols, dtype=jnp.int32)) % cols
    split = attended.reshape(attended.shape[0], rows, cols, block)
    split = jnp.take(jnp.take(split, row_order, axis=1), col_order, axis=2)
    return jnp.dot(
        split.reshape(attended.shape[0], -1),
        gathered.reshape(rows * cols * block, -1),
        preferred_element_type=jnp.float32,
    )


def hidden_product(block, gate_part, up_part, down_part):
    contract = (((1,), (1,)), ((), ()))
    gate_value = lax.dot_general(block, gate_part, contract, preferred_element_type=jnp.float32)
    up_value = lax.dot_general(block, up_part, contract, preferred_element_type=jnp.float32)
    active = (jax.nn.silu(gate_value) * up_value).astype(jnp.bfloat16)
    return jnp.dot(active, down_part, preferred_element_type=jnp.float32)


def expert_output(work_rows, gate_part, up_part, down_part):
    return hidden_product(work_rows, gate_part, up_part, down_part)


def local(
    query_rows,
    key_rows,
    value_rows,
    residual,
    document_owner,
    document_length,
    document_offset,
    query_gain,
    key_gain,
    output_weight,
    post_gain,
    routes,
    route_weight,
    gate_weight,
    up_weight,
    down_weight,
):
    owner_total = lax.axis_size("dp")
    expert_total = lax.axis_size("expert")
    row_total = query_rows.shape[0]
    capacity = row_total * 3 // (2 * owner_total)
    owners = document_owner[0]
    lengths = document_length[0]
    offsets = document_offset[0]
    starts = jnp.cumsum(lengths) - lengths
    owner_ids = jnp.arange(owner_total, dtype=jnp.int32)
    matches = owners[None, :] == owner_ids[:, None]
    start_of = jnp.sum(jnp.where(matches, starts[None, :], 0), axis=1)
    length_of = jnp.sum(jnp.where(matches, lengths[None, :], 0), axis=1)
    offset_of = jnp.sum(jnp.where(matches, offsets[None, :], 0), axis=1)
    slot_ids = jnp.arange(capacity, dtype=jnp.int32)
    source_rows = jnp.minimum(start_of[:, None] + slot_ids[None, :], row_total - 1).reshape(-1)
    pack_slot = jnp.where(
        slot_ids[None, :] < length_of[:, None], offset_of[:, None] + slot_ids[None, :], -1
    )
    total_slots = owner_total * capacity
    flat_slots = jnp.arange(total_slots, dtype=jnp.int32)
    pack_ids = jnp.arange(row_total, dtype=jnp.int32)
    whole_rows = jnp.concatenate([query_rows, key_rows, value_rows, residual], axis=1)
    widths = [query_rows.shape[1], key_rows.shape[1], value_rows.shape[1], residual.shape[1]]
    data_width = sum(widths)
    slot_column = jnp.broadcast_to(
        pack_slot.reshape(-1, 1).astype(jnp.bfloat16), (total_slots, 128)
    )
    outgoing_pack = jnp.concatenate([whole_rows[source_rows], slot_column], axis=1)
    got = lax.all_to_all(
        outgoing_pack.reshape(owner_total, capacity, -1),
        "dp",
        split_axis=0,
        concat_axis=0,
        tiled=True,
    ).reshape(total_slots, -1)
    got_slot = got[:, data_width].astype(jnp.int32)
    placed = got_slot[None, :] == pack_ids[:, None]
    slot_of = jnp.sum(jnp.where(placed, flat_slots[None, :], 0), axis=1)
    packed = got[slot_of]
    bounds = [0]
    for width in widths:
        bounds.append(bounds[-1] + width)
    pack_query, pack_key, pack_value, pack_residual = (
        packed[:, bounds[i] : bounds[i + 1]] for i in range(4)
    )
    identity = slot_of // capacity
    position = slot_of % capacity
    attended = attend(pack_query, pack_key, pack_value, identity, position, query_gain, key_gain)
    hidden_state = pack_residual.astype(jnp.float32) + project_heads(attended, output_weight)
    normed = rms_scale(hidden_state, post_gain).astype(jnp.bfloat16)
    top_total = routes.shape[1]
    most = row_total * top_total * 5 // (4 * expert_total)
    expert_ids = jnp.arange(expert_total, dtype=jnp.int32)
    routed = routes[:, :, None] == expert_ids[None, None, :]
    chosen = jnp.sum(routed.astype(jnp.int32), axis=1)
    earlier = (pack_ids[None, :] < pack_ids[:, None]).astype(jnp.int32)
    rank = jnp.dot(earlier, chosen)
    ranked = jnp.where(chosen > 0, rank, -1)
    place_ids = jnp.arange(most, dtype=jnp.int32)
    hits = ranked.T[:, :, None] == place_ids[None, None, :]
    source_token = jnp.sum(jnp.where(hits, pack_ids[None, :, None], 0), axis=1)
    outgoing = normed[source_token.reshape(-1)].reshape(expert_total, most, -1)
    total_rows = expert_total * most
    received = lax.all_to_all(outgoing, "expert", split_axis=0, concat_axis=0, tiled=True)
    work_rows = received.reshape(total_rows, -1)
    gate_whole, up_whole, down_whole = (
        lax.all_gather(gate_weight, "dp", axis=1, tiled=True),
        lax.all_gather(up_weight, "dp", axis=1, tiled=True),
        lax.all_gather(down_weight, "dp", axis=1, tiled=True),
    )
    produced = expert_output(work_rows, gate_whole[0], up_whole[0], down_whole[0])
    produced = produced.astype(jnp.bfloat16)
    out_slots = produced.reshape(expert_total, most, -1)
    returned = lax.all_to_all(out_slots, "expert", split_axis=0, concat_axis=0, tiled=True)
    flat_back = returned.reshape(total_rows, -1)
    copy_rank = jnp.sum(jnp.where(routed, rank[:, None, :], 0), axis=2)
    copy_index = routes * most + copy_rank
    gates = route_weight / jnp.sum(route_weight, axis=1, keepdims=True)
    mixture = jnp.zeros(hidden_state.shape, jnp.float32)
    for route_slot in range(top_total):
        mixture = mixture + gates[:, route_slot : route_slot + 1] * flat_back[
            copy_index[:, route_slot]
        ].astype(jnp.float32)
    return (hidden_state + mixture).astype(jnp.bfloat16)


def solution(mesh):
    placed = (
        P(("dp", "expert"), None),
        P(("dp", "expert"), None),
        P(("dp", "expert"), None),
        P(("dp", "expert"), None),
        P(("dp", "expert"), None),
        P(("dp", "expert"), None),
        P(("dp", "expert"), None),
        P(),
        P(),
        P("expert", None),
        P(),
        P(("dp", "expert"), None),
        P(("dp", "expert"), None),
        P("expert", "dp", None),
        P("expert", "dp", None),
        P("expert", "dp", None),
    )
    return jax.shard_map(
        local, mesh=mesh, in_specs=placed, out_specs=P(("dp", "expert"), None), check_vma=False
    )
```

```python
import jax
import jax.numpy as jnp
from jax import lax
from jax.sharding import PartitionSpec as P

norm_epsilon = 1e-06
rope_base = 1000000.0


def rms_scale(values, gain):
    mean_square = jnp.mean(values * values, axis=-1, keepdims=True)
    return values * lax.rsqrt(mean_square + norm_epsilon) * gain


def rotary(values, positions):
    head_width = values.shape[-1]
    half_width = head_width // 2
    frequency = rope_base ** (-2.0 * jnp.arange(half_width, dtype=jnp.float32) / head_width)
    angles = positions.astype(jnp.float32)[:, None] * frequency[None, :]
    cosine_part = jnp.cos(angles)[:, None, :]
    sine_part = jnp.sin(angles)[:, None, :]
    leading = values[..., :half_width]
    trailing = values[..., half_width:]
    return jnp.concatenate(
        [
            leading * cosine_part - trailing * sine_part,
            trailing * cosine_part + leading * sine_part,
        ],
        axis=-1,
    )


def attend(query_part, key_part, value_part, identity, position, query_gain, key_gain):
    row_total = query_part.shape[0]
    head_width = query_gain.shape[0]
    head_count = query_part.shape[1] // head_width
    key_heads = key_part.shape[1] // head_width
    group_size = head_count // key_heads
    queries = rotary(
        rms_scale(
            query_part.reshape(row_total, head_count, head_width).astype(jnp.float32), query_gain
        ),
        position,
    ).astype(jnp.bfloat16)
    keys_normed = rotary(
        rms_scale(key_part.reshape(row_total, key_heads, head_width).astype(jnp.float32), key_gain),
        position,
    ).astype(jnp.bfloat16)
    queries = queries.reshape(row_total, key_heads, group_size, head_width)
    scores = jnp.einsum(
        "pkgd,qkd->kgpq", queries, keys_normed, preferred_element_type=jnp.float32
    ) * head_width ** (-0.5)
    allowed = (identity[:, None] == identity[None, :]) & (position[None, :] <= position[:, None])
    scores = jnp.where(allowed, scores, -jnp.inf)
    largest = jnp.max(scores, axis=-1, keepdims=True)
    powers = jnp.exp(scores - largest)
    weights = (powers / jnp.sum(powers, axis=-1, keepdims=True)).astype(jnp.bfloat16)
    values_heads = value_part.reshape(row_total, key_heads, head_width)
    mixed = jnp.einsum("kgpq,qkd->pkgd", weights, values_heads, preferred_element_type=jnp.float32)
    return mixed.astype(jnp.bfloat16).reshape(row_total, head_count * head_width)


def ring_pairs(rows, cols, step_row, step_col):
    return [
        (r * cols + c, ((r + step_row) % rows) * cols + (c + step_col) % cols)
        for r in range(rows)
        for c in range(cols)
    ]


def ring_gather(block, rows, cols):
    up = lax.ppermute(block, "expert", ring_pairs(rows, cols, 1, 0))
    down = lax.ppermute(block, "expert", ring_pairs(rows, cols, -1, 0))
    up_two = lax.ppermute(up, "expert", ring_pairs(rows, cols, 1, 0))
    by_row = jnp.stack([block, down, up_two, up])
    relative = {0: by_row}
    right = by_row
    left = by_row
    half = cols // 2
    for step in range(1, half + 1):
        right = lax.ppermute(right, "expert", ring_pairs(rows, cols, 0, 1))
        relative[-step % cols] = right
        if step < half:
            left = lax.ppermute(left, "expert", ring_pairs(rows, cols, 0, -1))
            relative[step] = left
    return jnp.stack([relative[k] for k in range(cols)], axis=1)


def spread_over_dp(piece, ring, cores):
    dp_pairs = lambda shift: [
        (r * cores + c, ((r + shift) % ring) * cores + c) for r in range(ring) for c in range(cores)
    ]
    other = lax.ppermute(piece, "dp", [(i, i ^ 1) for i in range(ring * cores)])
    pair = jnp.stack([piece, other])
    up = lax.ppermute(pair, "dp", dp_pairs(1))
    down = lax.ppermute(pair, "dp", dp_pairs(-1))
    up_two = lax.ppermute(up, "dp", dp_pairs(1))
    return jnp.stack([pair, down, up_two, up])


def project_heads(attended, output_weight):
    expert_total = lax.axis_size("expert")
    owner_total = lax.axis_size("dp")
    cols = 16
    rows = expert_total // cols
    block = output_weight.shape[0]
    if rows != 4 or expert_total % cols or owner_total != 8 or block % owner_total:
        return jnp.dot(
            attended,
            lax.all_gather(output_weight, "expert", axis=0, tiled=True),
            preferred_element_type=jnp.float32,
        )
    ring, cores = 4, 2
    share = block // owner_total
    own = lax.axis_index("expert")
    own_row = own // cols
    own_col = own % cols
    own_dp = lax.axis_index("dp")
    own_x = own_dp // cores
    own_core = own_dp % cores
    piece = lax.dynamic_slice_in_dim(output_weight, own_dp * share, share, 0)
    gathered = spread_over_dp(ring_gather(piece, rows, cols), ring, cores)
    steps = jnp.arange
    x_src = (own_x + steps(ring, dtype=jnp.int32)) % ring
    core_src = own_core ^ steps(cores, dtype=jnp.int32)
    row_src = (own_row + steps(rows, dtype=jnp.int32)) % rows
    col_src = (own_col + steps(cols, dtype=jnp.int32)) % cols
    dp_src = x_src[:, None] * cores + core_src[None, :]
    block_src = row_src[:, None] * cols + col_src[None, :]
    column = (
        block_src[None, None, :, :, None] * block
        + dp_src[:, :, None, None, None] * share
        + steps(share, dtype=jnp.int32)[None, None, None, None, :]
    ).reshape(-1)
    return jnp.dot(
        jnp.take(attended, column, axis=1),
        gathered.reshape(column.shape[0], -1),
        preferred_element_type=jnp.float32,
    )


def hidden_product(block, gate_part, up_part, down_part):
    contract = (((1,), (1,)), ((), ()))
    gate_value = lax.dot_general(block, gate_part, contract, preferred_element_type=jnp.float32)
    up_value = lax.dot_general(block, up_part, contract, preferred_element_type=jnp.float32)
    active = (jax.nn.silu(gate_value) * up_value).astype(jnp.bfloat16)
    return jnp.dot(active, down_part, preferred_element_type=jnp.float32)


def expert_output(work_rows, gate_part, up_part, down_part):
    return hidden_product(work_rows, gate_part, up_part, down_part)


def local(
    query_rows,
    key_rows,
    value_rows,
    residual,
    document_owner,
    document_length,
    document_offset,
    query_gain,
    key_gain,
    output_weight,
    post_gain,
    routes,
    route_weight,
    gate_weight,
    up_weight,
    down_weight,
):
    owner_total = lax.axis_size("dp")
    expert_total = lax.axis_size("expert")
    row_total = query_rows.shape[0]
    capacity = row_total * 3 // (2 * owner_total)
    owners = document_owner[0]
    lengths = document_length[0]
    offsets = document_offset[0]
    starts = jnp.cumsum(lengths) - lengths
    owner_ids = jnp.arange(owner_total, dtype=jnp.int32)
    matches = owners[None, :] == owner_ids[:, None]
    start_of = jnp.sum(jnp.where(matches, starts[None, :], 0), axis=1)
    length_of = jnp.sum(jnp.where(matches, lengths[None, :], 0), axis=1)
    offset_of = jnp.sum(jnp.where(matches, offsets[None, :], 0), axis=1)
    slot_ids = jnp.arange(capacity, dtype=jnp.int32)
    source_rows = jnp.minimum(start_of[:, None] + slot_ids[None, :], row_total - 1).reshape(-1)
    pack_slot = jnp.where(
        slot_ids[None, :] < length_of[:, None], offset_of[:, None] + slot_ids[None, :], -1
    )
    total_slots = owner_total * capacity
    flat_slots = jnp.arange(total_slots, dtype=jnp.int32)
    pack_ids = jnp.arange(row_total, dtype=jnp.int32)
    whole_rows = jnp.concatenate([query_rows, key_rows, value_rows, residual], axis=1)
    widths = [query_rows.shape[1], key_rows.shape[1], value_rows.shape[1], residual.shape[1]]
    data_width = sum(widths)
    slot_column = jnp.broadcast_to(
        pack_slot.reshape(-1, 1).astype(jnp.bfloat16), (total_slots, 128)
    )
    outgoing_pack = jnp.concatenate([whole_rows[source_rows], slot_column], axis=1)
    got = lax.all_to_all(
        outgoing_pack.reshape(owner_total, capacity, -1),
        "dp",
        split_axis=0,
        concat_axis=0,
        tiled=True,
    ).reshape(total_slots, -1)
    got_slot = got[:, data_width].astype(jnp.int32)
    placed = got_slot[None, :] == pack_ids[:, None]
    slot_of = jnp.sum(jnp.where(placed, flat_slots[None, :], 0), axis=1)
    packed = got[slot_of]
    bounds = [0]
    for width in widths:
        bounds.append(bounds[-1] + width)
    pack_query, pack_key, pack_value, pack_residual = (
        packed[:, bounds[i] : bounds[i + 1]] for i in range(4)
    )
    identity = slot_of // capacity
    position = slot_of % capacity
    attended = attend(pack_query, pack_key, pack_value, identity, position, query_gain, key_gain)
    hidden_state = pack_residual.astype(jnp.float32) + project_heads(attended, output_weight)
    normed = rms_scale(hidden_state, post_gain).astype(jnp.bfloat16)
    top_total = routes.shape[1]
    most = row_total * top_total * 5 // (4 * expert_total)
    expert_ids = jnp.arange(expert_total, dtype=jnp.int32)
    routed = routes[:, :, None] == expert_ids[None, None, :]
    chosen = jnp.sum(routed.astype(jnp.int32), axis=1)
    earlier = (pack_ids[None, :] < pack_ids[:, None]).astype(jnp.int32)
    rank = jnp.dot(earlier, chosen)
    ranked = jnp.where(chosen > 0, rank, -1)
    place_ids = jnp.arange(most, dtype=jnp.int32)
    hits = ranked.T[:, :, None] == place_ids[None, None, :]
    source_token = jnp.sum(jnp.where(hits, pack_ids[None, :, None], 0), axis=1)
    outgoing = normed[source_token.reshape(-1)].reshape(expert_total, most, -1)
    total_rows = expert_total * most
    received = lax.all_to_all(outgoing, "expert", split_axis=0, concat_axis=0, tiled=True)
    work_rows = received.reshape(total_rows, -1)
    gate_whole, up_whole, down_whole = (
        lax.all_gather(gate_weight, "dp", axis=1, tiled=True),
        lax.all_gather(up_weight, "dp", axis=1, tiled=True),
        lax.all_gather(down_weight, "dp", axis=1, tiled=True),
    )
    produced = expert_output(work_rows, gate_whole[0], up_whole[0], down_whole[0])
    produced = produced.astype(jnp.bfloat16)
    out_slots = produced.reshape(expert_total, most, -1)
    returned = lax.all_to_all(out_slots, "expert", split_axis=0, concat_axis=0, tiled=True)
    flat_back = returned.reshape(total_rows, -1)
    copy_rank = jnp.sum(jnp.where(routed, rank[:, None, :], 0), axis=2)
    copy_index = routes * most + copy_rank
    gates = route_weight / jnp.sum(route_weight, axis=1, keepdims=True)
    mixture = jnp.zeros(hidden_state.shape, jnp.float32)
    for route_slot in range(top_total):
        mixture = mixture + gates[:, route_slot : route_slot + 1] * flat_back[
            copy_index[:, route_slot]
        ].astype(jnp.float32)
    return (hidden_state + mixture).astype(jnp.bfloat16)


def solution(mesh):
    placed = (
        P(("dp", "expert"), None),
        P(("dp", "expert"), None),
        P(("dp", "expert"), None),
        P(("dp", "expert"), None),
        P(("dp", "expert"), None),
        P(("dp", "expert"), None),
        P(("dp", "expert"), None),
        P(),
        P(),
        P("expert", None),
        P(),
        P(("dp", "expert"), None),
        P(("dp", "expert"), None),
        P("expert", "dp", None),
        P("expert", "dp", None),
        P("expert", "dp", None),
    )
    return jax.shard_map(
        local, mesh=mesh, in_specs=placed, out_specs=P(("dp", "expert"), None), check_vma=False
    )
```

```python
import jax
import jax.numpy as jnp
from jax import lax
from jax.sharding import PartitionSpec as P

norm_epsilon = 1e-06
rope_base = 1000000.0


def rms_scale(values, gain):
    mean_square = jnp.mean(values * values, axis=-1, keepdims=True)
    return values * lax.rsqrt(mean_square + norm_epsilon) * gain


def rotary(values, positions):
    head_width = values.shape[-1]
    half_width = head_width // 2
    frequency = rope_base ** (-2.0 * jnp.arange(half_width, dtype=jnp.float32) / head_width)
    angles = positions.astype(jnp.float32)[:, None] * frequency[None, :]
    cosine_part = jnp.cos(angles)[:, None, :]
    sine_part = jnp.sin(angles)[:, None, :]
    leading = values[..., :half_width]
    trailing = values[..., half_width:]
    return jnp.concatenate(
        [
            leading * cosine_part - trailing * sine_part,
            trailing * cosine_part + leading * sine_part,
        ],
        axis=-1,
    )


def attend(query_part, key_part, value_part, identity, position, query_gain, key_gain):
    row_total = query_part.shape[0]
    head_width = query_gain.shape[0]
    head_count = query_part.shape[1] // head_width
    key_heads = key_part.shape[1] // head_width
    group_size = head_count // key_heads
    queries = rotary(
        rms_scale(
            query_part.reshape(row_total, head_count, head_width).astype(jnp.float32), query_gain
        ),
        position,
    ).astype(jnp.bfloat16)
    keys_normed = rotary(
        rms_scale(key_part.reshape(row_total, key_heads, head_width).astype(jnp.float32), key_gain),
        position,
    ).astype(jnp.bfloat16)
    queries = queries.reshape(row_total, key_heads, group_size, head_width)
    scores = jnp.einsum(
        "pkgd,qkd->kgpq", queries, keys_normed, preferred_element_type=jnp.float32
    ) * head_width ** (-0.5)
    allowed = (identity[:, None] == identity[None, :]) & (position[None, :] <= position[:, None])
    scores = jnp.where(allowed, scores, -jnp.inf)
    largest = jnp.max(scores, axis=-1, keepdims=True)
    powers = jnp.exp(scores - largest)
    weights = (powers / jnp.sum(powers, axis=-1, keepdims=True)).astype(jnp.bfloat16)
    values_heads = value_part.reshape(row_total, key_heads, head_width)
    mixed = jnp.einsum("kgpq,qkd->pkgd", weights, values_heads, preferred_element_type=jnp.float32)
    return mixed.astype(jnp.bfloat16).reshape(row_total, head_count * head_width)


def ring_pairs(rows, cols, step_row, step_col):
    return [
        (r * cols + c, ((r + step_row) % rows) * cols + (c + step_col) % cols)
        for r in range(rows)
        for c in range(cols)
    ]


def ring_gather(block, rows, cols):
    up = lax.ppermute(block, "expert", ring_pairs(rows, cols, 1, 0))
    down = lax.ppermute(block, "expert", ring_pairs(rows, cols, -1, 0))
    up_two = lax.ppermute(up, "expert", ring_pairs(rows, cols, 1, 0))
    by_row = jnp.stack([block, down, up_two, up])
    relative = {0: by_row}
    right = by_row
    left = by_row
    half = cols // 2
    for step in range(1, half + 1):
        right = lax.ppermute(right, "expert", ring_pairs(rows, cols, 0, 1))
        relative[-step % cols] = right
        if step < half:
            left = lax.ppermute(left, "expert", ring_pairs(rows, cols, 0, -1))
            relative[step] = left
    return jnp.stack([relative[k] for k in range(cols)], axis=1)


def project_heads(attended, output_weight):
    expert_total = lax.axis_size("expert")
    cols = 16
    rows = expert_total // cols
    if rows != 4 or expert_total % cols:
        return jnp.dot(
            attended,
            lax.all_gather(output_weight, "expert", axis=0, tiled=True),
            preferred_element_type=jnp.float32,
        )
    own = lax.axis_index("expert")
    own_row = own // cols
    own_col = own % cols
    gathered = ring_gather(output_weight, rows, cols)
    block = output_weight.shape[0]
    row_order = (own_row + jnp.arange(rows, dtype=jnp.int32)) % rows
    col_order = (own_col + jnp.arange(cols, dtype=jnp.int32)) % cols
    split = attended.reshape(attended.shape[0], rows, cols, block)
    split = jnp.take(jnp.take(split, row_order, axis=1), col_order, axis=2)
    return jnp.dot(
        split.reshape(attended.shape[0], -1),
        gathered.reshape(rows * cols * block, -1),
        preferred_element_type=jnp.float32,
    )


def hidden_product(block, gate_part, up_part, down_part):
    contract = (((1,), (1,)), ((), ()))
    gate_value = lax.dot_general(block, gate_part, contract, preferred_element_type=jnp.float32)
    up_value = lax.dot_general(block, up_part, contract, preferred_element_type=jnp.float32)
    active = (jax.nn.silu(gate_value) * up_value).astype(jnp.bfloat16)
    return jnp.dot(active, down_part, preferred_element_type=jnp.float32)


def expert_output(work_rows, gate_part, up_part, down_part):
    return hidden_product(work_rows, gate_part, up_part, down_part)


def local(
    query_rows,
    key_rows,
    value_rows,
    residual,
    document_owner,
    document_length,
    document_offset,
    query_gain,
    key_gain,
    output_weight,
    post_gain,
    routes,
    route_weight,
    gate_weight,
    up_weight,
    down_weight,
):
    owner_total = lax.axis_size("dp")
    expert_total = lax.axis_size("expert")
    row_total = query_rows.shape[0]
    capacity = row_total * 3 // (2 * owner_total)
    owners = document_owner[0]
    lengths = document_length[0]
    offsets = document_offset[0]
    starts = jnp.cumsum(lengths) - lengths
    owner_ids = jnp.arange(owner_total, dtype=jnp.int32)
    matches = owners[None, :] == owner_ids[:, None]
    start_of = jnp.sum(jnp.where(matches, starts[None, :], 0), axis=1)
    length_of = jnp.sum(jnp.where(matches, lengths[None, :], 0), axis=1)
    offset_of = jnp.sum(jnp.where(matches, offsets[None, :], 0), axis=1)
    slot_ids = jnp.arange(capacity, dtype=jnp.int32)
    source_rows = jnp.minimum(start_of[:, None] + slot_ids[None, :], row_total - 1).reshape(-1)
    pack_slot = jnp.where(
        slot_ids[None, :] < length_of[:, None], offset_of[:, None] + slot_ids[None, :], -1
    )
    total_slots = owner_total * capacity
    flat_slots = jnp.arange(total_slots, dtype=jnp.int32)
    pack_ids = jnp.arange(row_total, dtype=jnp.int32)
    whole_rows = jnp.concatenate([query_rows, key_rows, value_rows, residual], axis=1)
    widths = [query_rows.shape[1], key_rows.shape[1], value_rows.shape[1], residual.shape[1]]
    data_width = sum(widths)
    slot_column = jnp.broadcast_to(
        pack_slot.reshape(-1, 1).astype(jnp.bfloat16), (total_slots, 128)
    )
    outgoing_pack = jnp.concatenate([whole_rows[source_rows], slot_column], axis=1)
    got = lax.all_to_all(
        outgoing_pack.reshape(owner_total, capacity, -1),
        "dp",
        split_axis=0,
        concat_axis=0,
        tiled=True,
    ).reshape(total_slots, -1)
    got_slot = got[:, data_width].astype(jnp.int32)
    placed = got_slot[None, :] == pack_ids[:, None]
    slot_of = jnp.sum(jnp.where(placed, flat_slots[None, :], 0), axis=1)
    packed = got[slot_of]
    bounds = [0]
    for width in widths:
        bounds.append(bounds[-1] + width)
    pack_query, pack_key, pack_value, pack_residual = (
        packed[:, bounds[i] : bounds[i + 1]] for i in range(4)
    )
    identity = slot_of // capacity
    position = slot_of % capacity
    attended = attend(pack_query, pack_key, pack_value, identity, position, query_gain, key_gain)
    hidden_state = pack_residual.astype(jnp.float32) + project_heads(attended, output_weight)
    normed = rms_scale(hidden_state, post_gain).astype(jnp.bfloat16)
    top_total = routes.shape[1]
    most = row_total * top_total * 5 // (4 * expert_total)
    expert_ids = jnp.arange(expert_total, dtype=jnp.int32)
    routed = routes[:, :, None] == expert_ids[None, None, :]
    chosen = jnp.sum(routed.astype(jnp.int32), axis=1)
    earlier = (pack_ids[None, :] < pack_ids[:, None]).astype(jnp.int32)
    rank = jnp.dot(earlier, chosen)
    ranked = jnp.where(chosen > 0, rank, -1)
    place_ids = jnp.arange(most, dtype=jnp.int32)
    hits = ranked.T[:, :, None] == place_ids[None, None, :]
    source_token = jnp.sum(jnp.where(hits, pack_ids[None, :, None], 0), axis=1)
    outgoing = normed[source_token.reshape(-1)].reshape(expert_total, most, -1)
    total_rows = expert_total * most
    gate_whole, up_whole, down_whole = (
        lax.all_gather(gate_weight, "dp", axis=1, tiled=True),
        lax.all_gather(up_weight, "dp", axis=1, tiled=True),
        lax.all_gather(down_weight, "dp", axis=1, tiled=True),
    )
    chunks = 2
    chunk = most // chunks
    pieces = []
    for part in range(chunks):
        received = lax.all_to_all(
            outgoing[:, part * chunk : (part + 1) * chunk],
            "expert",
            split_axis=0,
            concat_axis=0,
            tiled=True,
        )
        produced = expert_output(
            received.reshape(expert_total * chunk, -1), gate_whole[0], up_whole[0], down_whole[0]
        ).astype(jnp.bfloat16)
        pieces.append(
            lax.all_to_all(
                produced.reshape(expert_total, chunk, -1),
                "expert",
                split_axis=0,
                concat_axis=0,
                tiled=True,
            )
        )
    returned = jnp.concatenate(pieces, axis=1)
    flat_back = returned.reshape(total_rows, -1)
    copy_rank = jnp.sum(jnp.where(routed, rank[:, None, :], 0), axis=2)
    copy_index = routes * most + copy_rank
    gates = route_weight / jnp.sum(route_weight, axis=1, keepdims=True)
    mixture = jnp.zeros(hidden_state.shape, jnp.float32)
    for route_slot in range(top_total):
        mixture = mixture + gates[:, route_slot : route_slot + 1] * flat_back[
            copy_index[:, route_slot]
        ].astype(jnp.float32)
    return (hidden_state + mixture).astype(jnp.bfloat16)


def solution(mesh):
    placed = (
        P(("dp", "expert"), None),
        P(("dp", "expert"), None),
        P(("dp", "expert"), None),
        P(("dp", "expert"), None),
        P(("dp", "expert"), None),
        P(("dp", "expert"), None),
        P(("dp", "expert"), None),
        P(),
        P(),
        P("expert", None),
        P(),
        P(("dp", "expert"), None),
        P(("dp", "expert"), None),
        P("expert", "dp", None),
        P("expert", "dp", None),
        P("expert", "dp", None),
    )
    return jax.shard_map(
        local, mesh=mesh, in_specs=placed, out_specs=P(("dp", "expert"), None), check_vma=False
    )
```

```python
import jax
import jax.numpy as jnp
from jax import lax
from jax.sharding import PartitionSpec as P

norm_epsilon = 1e-06
rope_base = 1000000.0


def rms_scale(values, gain):
    mean_square = jnp.mean(values * values, axis=-1, keepdims=True)
    return values * lax.rsqrt(mean_square + norm_epsilon) * gain


def rotary(values, positions):
    head_width = values.shape[-1]
    half_width = head_width // 2
    frequency = rope_base ** (-2.0 * jnp.arange(half_width, dtype=jnp.float32) / head_width)
    angles = positions.astype(jnp.float32)[:, None] * frequency[None, :]
    cosine_part = jnp.cos(angles)[:, None, :]
    sine_part = jnp.sin(angles)[:, None, :]
    leading = values[..., :half_width]
    trailing = values[..., half_width:]
    return jnp.concatenate(
        [
            leading * cosine_part - trailing * sine_part,
            trailing * cosine_part + leading * sine_part,
        ],
        axis=-1,
    )


def attend(query_part, key_part, value_part, identity, position, query_gain, key_gain):
    row_total = query_part.shape[0]
    head_width = query_gain.shape[0]
    head_count = query_part.shape[1] // head_width
    key_heads = key_part.shape[1] // head_width
    group_size = head_count // key_heads
    queries = rotary(
        rms_scale(
            query_part.reshape(row_total, head_count, head_width).astype(jnp.float32), query_gain
        ),
        position,
    ).astype(jnp.bfloat16)
    keys_normed = rotary(
        rms_scale(key_part.reshape(row_total, key_heads, head_width).astype(jnp.float32), key_gain),
        position,
    ).astype(jnp.bfloat16)
    queries = queries.reshape(row_total, key_heads, group_size, head_width)
    scores = jnp.einsum(
        "pkgd,qkd->kgpq", queries, keys_normed, preferred_element_type=jnp.float32
    ) * head_width ** (-0.5)
    allowed = (identity[:, None] == identity[None, :]) & (position[None, :] <= position[:, None])
    scores = jnp.where(allowed, scores, -jnp.inf)
    largest = jnp.max(scores, axis=-1, keepdims=True)
    powers = jnp.exp(scores - largest)
    weights = (powers / jnp.sum(powers, axis=-1, keepdims=True)).astype(jnp.bfloat16)
    values_heads = value_part.reshape(row_total, key_heads, head_width)
    mixed = jnp.einsum("kgpq,qkd->pkgd", weights, values_heads, preferred_element_type=jnp.float32)
    return mixed.astype(jnp.bfloat16).reshape(row_total, head_count * head_width)


def ring_pairs(rows, cols, step_row, step_col):
    return [
        (r * cols + c, ((r + step_row) % rows) * cols + (c + step_col) % cols)
        for r in range(rows)
        for c in range(cols)
    ]


def ring_gather(block, rows, cols, owners):
    expert_total = rows * cols
    up = lax.ppermute(block, "expert", ring_pairs(rows, cols, 1, 0))
    down = lax.ppermute(block, "expert", ring_pairs(rows, cols, -1, 0))
    up_two = lax.ppermute(up, "expert", ring_pairs(rows, cols, 1, 0))
    by_row = jnp.stack([block, down, up_two, up])
    walk = [
        (owner * expert_total + src, owner * expert_total + dst)
        for owner in range(owners)
        for src, dst in ring_pairs(rows, cols, 0, 1 if owner % 2 == 0 else -1)
    ]
    half = cols // 2
    mine = []
    current = by_row
    for step in range(half):
        current = lax.ppermute(current, ("dp", "expert"), walk)
        mine.append(current)
    mine = jnp.stack(mine)
    partner = lax.ppermute(mine[: half - 1], "dp", [(i, i ^ 1) for i in range(owners)])
    return jnp.concatenate([by_row[None], mine, partner], axis=0)


def project_heads(attended, output_weight):
    expert_total = lax.axis_size("expert")
    owner_total = lax.axis_size("dp")
    cols = 16
    rows = expert_total // cols
    if rows != 4 or expert_total % cols or owner_total % 2:
        return jnp.dot(
            attended,
            lax.all_gather(output_weight, "expert", axis=0, tiled=True),
            preferred_element_type=jnp.float32,
        )
    own = lax.axis_index("expert")
    own_row = own // cols
    own_col = own % cols
    sign = 1 - 2 * (lax.axis_index("dp") % 2)
    half = cols // 2
    steps = jnp.arange(1, half + 1, dtype=jnp.int32)
    offsets = jnp.concatenate(
        [jnp.zeros((1,), jnp.int32), -sign * steps, sign * steps[: half - 1]]
    )
    gathered = ring_gather(output_weight, rows, cols, owner_total)
    block = output_weight.shape[0]
    row_order = (own_row + jnp.arange(rows, dtype=jnp.int32)) % rows
    col_order = (own_col + offsets) % cols
    split = attended.reshape(attended.shape[0], rows, cols, block)
    split = jnp.take(jnp.take(split, col_order, axis=2), row_order, axis=1)
    split = jnp.swapaxes(split, 1, 2)
    return jnp.dot(
        split.reshape(attended.shape[0], -1),
        gathered.reshape(rows * cols * block, -1),
        preferred_element_type=jnp.float32,
    )


def hidden_product(block, gate_part, up_part, down_part):
    contract = (((1,), (1,)), ((), ()))
    gate_value = lax.dot_general(block, gate_part, contract, preferred_element_type=jnp.float32)
    up_value = lax.dot_general(block, up_part, contract, preferred_element_type=jnp.float32)
    active = (jax.nn.silu(gate_value) * up_value).astype(jnp.bfloat16)
    return jnp.dot(active, down_part, preferred_element_type=jnp.float32)


def expert_output(work_rows, gate_part, up_part, down_part):
    return hidden_product(work_rows, gate_part, up_part, down_part)


def local(
    query_rows,
    key_rows,
    value_rows,
    residual,
    document_owner,
    document_length,
    document_offset,
    query_gain,
    key_gain,
    output_weight,
    post_gain,
    routes,
    route_weight,
    gate_weight,
    up_weight,
    down_weight,
):
    owner_total = lax.axis_size("dp")
    expert_total = lax.axis_size("expert")
    row_total = query_rows.shape[0]
    capacity = row_total * 3 // (2 * owner_total)
    owners = document_owner[0]
    lengths = document_length[0]
    offsets = document_offset[0]
    starts = jnp.cumsum(lengths) - lengths
    owner_ids = jnp.arange(owner_total, dtype=jnp.int32)
    matches = owners[None, :] == owner_ids[:, None]
    start_of = jnp.sum(jnp.where(matches, starts[None, :], 0), axis=1)
    length_of = jnp.sum(jnp.where(matches, lengths[None, :], 0), axis=1)
    offset_of = jnp.sum(jnp.where(matches, offsets[None, :], 0), axis=1)
    slot_ids = jnp.arange(capacity, dtype=jnp.int32)
    source_rows = jnp.minimum(start_of[:, None] + slot_ids[None, :], row_total - 1).reshape(-1)
    pack_slot = jnp.where(
        slot_ids[None, :] < length_of[:, None], offset_of[:, None] + slot_ids[None, :], -1
    )
    total_slots = owner_total * capacity
    flat_slots = jnp.arange(total_slots, dtype=jnp.int32)
    pack_ids = jnp.arange(row_total, dtype=jnp.int32)
    whole_rows = jnp.concatenate([query_rows, key_rows, value_rows, residual], axis=1)
    widths = [query_rows.shape[1], key_rows.shape[1], value_rows.shape[1], residual.shape[1]]
    data_width = sum(widths)
    slot_column = jnp.broadcast_to(
        pack_slot.reshape(-1, 1).astype(jnp.bfloat16), (total_slots, 128)
    )
    outgoing_pack = jnp.concatenate([whole_rows[source_rows], slot_column], axis=1)
    got = lax.all_to_all(
        outgoing_pack.reshape(owner_total, capacity, -1),
        "dp",
        split_axis=0,
        concat_axis=0,
        tiled=True,
    ).reshape(total_slots, -1)
    got_slot = got[:, data_width].astype(jnp.int32)
    placed = got_slot[None, :] == pack_ids[:, None]
    slot_of = jnp.sum(jnp.where(placed, flat_slots[None, :], 0), axis=1)
    packed = got[slot_of]
    bounds = [0]
    for width in widths:
        bounds.append(bounds[-1] + width)
    pack_query, pack_key, pack_value, pack_residual = (
        packed[:, bounds[i] : bounds[i + 1]] for i in range(4)
    )
    identity = slot_of // capacity
    position = slot_of % capacity
    attended = attend(pack_query, pack_key, pack_value, identity, position, query_gain, key_gain)
    hidden_state = pack_residual.astype(jnp.float32) + project_heads(attended, output_weight)
    normed = rms_scale(hidden_state, post_gain).astype(jnp.bfloat16)
    top_total = routes.shape[1]
    most = row_total * top_total * 5 // (4 * expert_total)
    expert_ids = jnp.arange(expert_total, dtype=jnp.int32)
    routed = routes[:, :, None] == expert_ids[None, None, :]
    chosen = jnp.sum(routed.astype(jnp.int32), axis=1)
    earlier = (pack_ids[None, :] < pack_ids[:, None]).astype(jnp.int32)
    rank = jnp.dot(earlier, chosen)
    ranked = jnp.where(chosen > 0, rank, -1)
    place_ids = jnp.arange(most, dtype=jnp.int32)
    hits = ranked.T[:, :, None] == place_ids[None, None, :]
    source_token = jnp.sum(jnp.where(hits, pack_ids[None, :, None], 0), axis=1)
    outgoing = normed[source_token.reshape(-1)].reshape(expert_total, most, -1)
    total_rows = expert_total * most
    received = lax.all_to_all(outgoing, "expert", split_axis=0, concat_axis=0, tiled=True)
    work_rows = received.reshape(total_rows, -1)
    gate_whole, up_whole, down_whole = (
        lax.all_gather(gate_weight, "dp", axis=1, tiled=True),
        lax.all_gather(up_weight, "dp", axis=1, tiled=True),
        lax.all_gather(down_weight, "dp", axis=1, tiled=True),
    )
    produced = expert_output(work_rows, gate_whole[0], up_whole[0], down_whole[0])
    produced = produced.astype(jnp.bfloat16)
    out_slots = produced.reshape(expert_total, most, -1)
    returned = lax.all_to_all(out_slots, "expert", split_axis=0, concat_axis=0, tiled=True)
    flat_back = returned.reshape(total_rows, -1)
    copy_rank = jnp.sum(jnp.where(routed, rank[:, None, :], 0), axis=2)
    copy_index = routes * most + copy_rank
    gates = route_weight / jnp.sum(route_weight, axis=1, keepdims=True)
    mixture = jnp.zeros(hidden_state.shape, jnp.float32)
    for route_slot in range(top_total):
        mixture = mixture + gates[:, route_slot : route_slot + 1] * flat_back[
            copy_index[:, route_slot]
        ].astype(jnp.float32)
    return (hidden_state + mixture).astype(jnp.bfloat16)


def solution(mesh):
    placed = (
        P(("dp", "expert"), None),
        P(("dp", "expert"), None),
        P(("dp", "expert"), None),
        P(("dp", "expert"), None),
        P(("dp", "expert"), None),
        P(("dp", "expert"), None),
        P(("dp", "expert"), None),
        P(),
        P(),
        P("expert", None),
        P(),
        P(("dp", "expert"), None),
        P(("dp", "expert"), None),
        P("expert", "dp", None),
        P("expert", "dp", None),
        P("expert", "dp", None),
    )
    return jax.shard_map(
        local, mesh=mesh, in_specs=placed, out_specs=P(("dp", "expert"), None), check_vma=False
    )
```

```python
import jax
import jax.numpy as jnp
from jax import lax
from jax.sharding import PartitionSpec as P

norm_epsilon = 1e-06
rope_base = 1000000.0


def rms_scale(values, gain):
    mean_square = jnp.mean(values * values, axis=-1, keepdims=True)
    return values * lax.rsqrt(mean_square + norm_epsilon) * gain


def rotary(values, positions):
    head_width = values.shape[-1]
    half_width = head_width // 2
    frequency = rope_base ** (-2.0 * jnp.arange(half_width, dtype=jnp.float32) / head_width)
    angles = positions.astype(jnp.float32)[:, None] * frequency[None, :]
    cosine_part = jnp.cos(angles)[:, None, :]
    sine_part = jnp.sin(angles)[:, None, :]
    leading = values[..., :half_width]
    trailing = values[..., half_width:]
    return jnp.concatenate(
        [
            leading * cosine_part - trailing * sine_part,
            trailing * cosine_part + leading * sine_part,
        ],
        axis=-1,
    )


def attend(query_part, key_part, value_part, identity, position, query_gain, key_gain):
    row_total = query_part.shape[0]
    head_width = query_gain.shape[0]
    head_count = query_part.shape[1] // head_width
    key_heads = key_part.shape[1] // head_width
    group_size = head_count // key_heads
    queries = rotary(
        rms_scale(
            query_part.reshape(row_total, head_count, head_width).astype(jnp.float32), query_gain
        ),
        position,
    ).astype(jnp.bfloat16)
    keys_normed = rotary(
        rms_scale(key_part.reshape(row_total, key_heads, head_width).astype(jnp.float32), key_gain),
        position,
    ).astype(jnp.bfloat16)
    queries = queries.reshape(row_total, key_heads, group_size, head_width)
    scores = jnp.einsum(
        "pkgd,qkd->kgpq", queries, keys_normed, preferred_element_type=jnp.float32
    ) * head_width ** (-0.5)
    allowed = (identity[:, None] == identity[None, :]) & (position[None, :] <= position[:, None])
    scores = jnp.where(allowed, scores, -jnp.inf)
    largest = jnp.max(scores, axis=-1, keepdims=True)
    powers = jnp.exp(scores - largest)
    weights = (powers / jnp.sum(powers, axis=-1, keepdims=True)).astype(jnp.bfloat16)
    values_heads = value_part.reshape(row_total, key_heads, head_width)
    mixed = jnp.einsum("kgpq,qkd->pkgd", weights, values_heads, preferred_element_type=jnp.float32)
    return mixed.astype(jnp.bfloat16).reshape(row_total, head_count * head_width)


def ring_pairs(rows, cols, step_row, step_col):
    return [
        (r * cols + c, ((r + step_row) % rows) * cols + (c + step_col) % cols)
        for r in range(rows)
        for c in range(cols)
    ]


def ring_gather(block, rows, cols, owners):
    expert_total = rows * cols
    up = lax.ppermute(block, "expert", ring_pairs(rows, cols, 1, 0))
    down = lax.ppermute(block, "expert", ring_pairs(rows, cols, -1, 0))
    up_two = lax.ppermute(up, "expert", ring_pairs(rows, cols, 1, 0))
    by_row = jnp.stack([block, down, up_two, up])
    walk = [
        (owner * expert_total + src, owner * expert_total + dst)
        for owner in range(owners)
        for src, dst in ring_pairs(rows, cols, 0, 1 if owner % 2 == 0 else -1)
    ]
    half = cols // 2
    mine = []
    current = by_row
    for step in range(half):
        current = lax.ppermute(current, ("dp", "expert"), walk)
        mine.append(current)
    mine = jnp.stack(mine)
    partner = lax.ppermute(mine[: half - 1], "dp", [(i, i ^ 1) for i in range(owners)])
    return jnp.concatenate([by_row[None], mine, partner], axis=0)


def project_heads(attended, output_weight):
    expert_total = lax.axis_size("expert")
    owner_total = lax.axis_size("dp")
    cols = 16
    rows = expert_total // cols
    if rows != 4 or expert_total % cols or owner_total % 2:
        return jnp.dot(
            attended,
            lax.all_gather(output_weight, "expert", axis=0, tiled=True),
            preferred_element_type=jnp.float32,
        )
    own = lax.axis_index("expert")
    own_row = own // cols
    own_col = own % cols
    sign = 1 - 2 * (lax.axis_index("dp") % 2)
    half = cols // 2
    steps = jnp.arange(1, half + 1, dtype=jnp.int32)
    offsets = jnp.concatenate(
        [jnp.zeros((1,), jnp.int32), -sign * steps, sign * steps[: half - 1]]
    )
    gathered = ring_gather(output_weight, rows, cols, owner_total)
    block = output_weight.shape[0]
    row_order = (own_row + jnp.arange(rows, dtype=jnp.int32)) % rows
    col_order = (own_col + offsets) % cols
    split = attended.reshape(attended.shape[0], rows, cols, block)
    split = jnp.take(jnp.take(split, col_order, axis=2), row_order, axis=1)
    split = jnp.swapaxes(split, 1, 2)
    return jnp.dot(
        split.reshape(attended.shape[0], -1),
        gathered.reshape(rows * cols * block, -1),
        preferred_element_type=jnp.float32,
    )


def hidden_product(block, gate_part, up_part, down_part):
    contract = (((1,), (1,)), ((), ()))
    gate_value = lax.dot_general(block, gate_part, contract, preferred_element_type=jnp.float32)
    up_value = lax.dot_general(block, up_part, contract, preferred_element_type=jnp.float32)
    active = (jax.nn.silu(gate_value) * up_value).astype(jnp.bfloat16)
    return jnp.dot(active, down_part, preferred_element_type=jnp.float32)


def expert_output(work_rows, gate_part, up_part, down_part):
    return hidden_product(work_rows, gate_part, up_part, down_part)


def local(
    query_rows,
    key_rows,
    value_rows,
    residual,
    document_owner,
    document_length,
    document_offset,
    query_gain,
    key_gain,
    output_weight,
    post_gain,
    routes,
    route_weight,
    gate_weight,
    up_weight,
    down_weight,
):
    owner_total = lax.axis_size("dp")
    expert_total = lax.axis_size("expert")
    row_total = query_rows.shape[0]
    capacity = row_total * 3 // (2 * owner_total)
    owners = document_owner[0]
    lengths = document_length[0]
    offsets = document_offset[0]
    starts = jnp.cumsum(lengths) - lengths
    owner_ids = jnp.arange(owner_total, dtype=jnp.int32)
    matches = owners[None, :] == owner_ids[:, None]
    start_of = jnp.sum(jnp.where(matches, starts[None, :], 0), axis=1)
    length_of = jnp.sum(jnp.where(matches, lengths[None, :], 0), axis=1)
    offset_of = jnp.sum(jnp.where(matches, offsets[None, :], 0), axis=1)
    slot_ids = jnp.arange(capacity, dtype=jnp.int32)
    source_rows = jnp.minimum(start_of[:, None] + slot_ids[None, :], row_total - 1).reshape(-1)
    pack_slot = jnp.where(
        slot_ids[None, :] < length_of[:, None], offset_of[:, None] + slot_ids[None, :], -1
    )
    total_slots = owner_total * capacity
    flat_slots = jnp.arange(total_slots, dtype=jnp.int32)
    pack_ids = jnp.arange(row_total, dtype=jnp.int32)
    whole_rows = jnp.concatenate([query_rows, key_rows, value_rows, residual], axis=1)
    widths = [query_rows.shape[1], key_rows.shape[1], value_rows.shape[1], residual.shape[1]]
    data_width = sum(widths)
    slot_column = jnp.broadcast_to(
        pack_slot.reshape(-1, 1).astype(jnp.bfloat16), (total_slots, 128)
    )
    outgoing_pack = jnp.concatenate([whole_rows[source_rows], slot_column], axis=1)
    got = lax.all_to_all(
        outgoing_pack.reshape(owner_total, capacity, -1),
        "dp",
        split_axis=0,
        concat_axis=0,
        tiled=True,
    ).reshape(total_slots, -1)
    got_slot = got[:, data_width].astype(jnp.int32)
    placed = got_slot[None, :] == pack_ids[:, None]
    slot_of = jnp.sum(jnp.where(placed, flat_slots[None, :], 0), axis=1)
    packed = got[slot_of]
    bounds = [0]
    for width in widths:
        bounds.append(bounds[-1] + width)
    pack_query, pack_key, pack_value, pack_residual = (
        packed[:, bounds[i] : bounds[i + 1]] for i in range(4)
    )
    identity = slot_of // capacity
    position = slot_of % capacity
    attended = attend(pack_query, pack_key, pack_value, identity, position, query_gain, key_gain)
    hidden_state = pack_residual.astype(jnp.float32) + project_heads(attended, output_weight)
    normed = rms_scale(hidden_state, post_gain).astype(jnp.bfloat16)
    top_total = routes.shape[1]
    most = row_total * top_total * 5 // (4 * expert_total)
    expert_ids = jnp.arange(expert_total, dtype=jnp.int32)
    routed = routes[:, :, None] == expert_ids[None, None, :]
    chosen = jnp.sum(routed.astype(jnp.int32), axis=1)
    earlier = (pack_ids[None, :] < pack_ids[:, None]).astype(jnp.int32)
    rank = jnp.dot(earlier, chosen)
    ranked = jnp.where(chosen > 0, rank, -1)
    place_ids = jnp.arange(most, dtype=jnp.int32)
    hits = ranked.T[:, :, None] == place_ids[None, None, :]
    source_token = jnp.sum(jnp.where(hits, pack_ids[None, :, None], 0), axis=1)
    picks = jnp.transpose(hits, (0, 2, 1)).reshape(-1, row_total).astype(jnp.bfloat16)
    outgoing = (
        jnp.dot(picks, normed, preferred_element_type=jnp.float32)
        .astype(jnp.bfloat16)
        .reshape(expert_total, most, -1)
    )
    total_rows = expert_total * most
    received = lax.all_to_all(outgoing, "expert", split_axis=0, concat_axis=0, tiled=True)
    work_rows = received.reshape(total_rows, -1)
    gate_whole, up_whole, down_whole = (
        lax.all_gather(gate_weight, "dp", axis=1, tiled=True),
        lax.all_gather(up_weight, "dp", axis=1, tiled=True),
        lax.all_gather(down_weight, "dp", axis=1, tiled=True),
    )
    produced = expert_output(work_rows, gate_whole[0], up_whole[0], down_whole[0])
    produced = produced.astype(jnp.bfloat16)
    out_slots = produced.reshape(expert_total, most, -1)
    returned = lax.all_to_all(out_slots, "expert", split_axis=0, concat_axis=0, tiled=True)
    flat_back = returned.reshape(total_rows, -1)
    copy_rank = jnp.sum(jnp.where(routed, rank[:, None, :], 0), axis=2)
    copy_index = routes * most + copy_rank
    gates = route_weight / jnp.sum(route_weight, axis=1, keepdims=True)
    slot_ids_back = jnp.arange(total_rows, dtype=jnp.int32)
    spread = jnp.sum(
        jnp.where(copy_index[:, :, None] == slot_ids_back[None, None, :], gates[:, :, None], 0.0),
        axis=1,
    )
    mixture = jnp.zeros(hidden_state.shape, jnp.float32)
    for _ in range(3):
        leading = lax.reduce_precision(spread, exponent_bits=8, mantissa_bits=7)
        spread = spread - leading
        part = leading.astype(jnp.bfloat16)
        mixture = mixture + jnp.dot(part, flat_back, preferred_element_type=jnp.float32)
    return (hidden_state + mixture).astype(jnp.bfloat16)


def solution(mesh):
    placed = (
        P(("dp", "expert"), None),
        P(("dp", "expert"), None),
        P(("dp", "expert"), None),
        P(("dp", "expert"), None),
        P(("dp", "expert"), None),
        P(("dp", "expert"), None),
        P(("dp", "expert"), None),
        P(),
        P(),
        P("expert", None),
        P(),
        P(("dp", "expert"), None),
        P(("dp", "expert"), None),
        P("expert", "dp", None),
        P("expert", "dp", None),
        P("expert", "dp", None),
    )
    return jax.shard_map(
        local, mesh=mesh, in_specs=placed, out_specs=P(("dp", "expert"), None), check_vma=False
    )
```

```python
import jax
import jax.numpy as jnp
from jax import lax
from jax.sharding import PartitionSpec as P

norm_epsilon = 1e-06
rope_base = 1000000.0


def rms_scale(values, gain):
    mean_square = jnp.mean(values * values, axis=-1, keepdims=True)
    return values * lax.rsqrt(mean_square + norm_epsilon) * gain


def rotary(values, positions):
    head_width = values.shape[-1]
    half_width = head_width // 2
    frequency = rope_base ** (-2.0 * jnp.arange(half_width, dtype=jnp.float32) / head_width)
    angles = positions.astype(jnp.float32)[:, None] * frequency[None, :]
    cosine_part = jnp.cos(angles)[:, None, :]
    sine_part = jnp.sin(angles)[:, None, :]
    leading = values[..., :half_width]
    trailing = values[..., half_width:]
    return jnp.concatenate(
        [
            leading * cosine_part - trailing * sine_part,
            trailing * cosine_part + leading * sine_part,
        ],
        axis=-1,
    )


def attend(query_part, key_part, value_part, identity, position, query_gain, key_gain):
    row_total = query_part.shape[0]
    head_width = query_gain.shape[0]
    head_count = query_part.shape[1] // head_width
    key_heads = key_part.shape[1] // head_width
    group_size = head_count // key_heads
    queries = rotary(
        rms_scale(
            query_part.reshape(row_total, head_count, head_width).astype(jnp.float32), query_gain
        ),
        position,
    ).astype(jnp.bfloat16)
    keys_normed = rotary(
        rms_scale(key_part.reshape(row_total, key_heads, head_width).astype(jnp.float32), key_gain),
        position,
    ).astype(jnp.bfloat16)
    queries = queries.reshape(row_total, key_heads, group_size, head_width)
    scores = jnp.einsum(
        "pkgd,qkd->kgpq", queries, keys_normed, preferred_element_type=jnp.float32
    ) * head_width ** (-0.5)
    allowed = (identity[:, None] == identity[None, :]) & (position[None, :] <= position[:, None])
    scores = jnp.where(allowed, scores, -jnp.inf)
    largest = jnp.max(scores, axis=-1, keepdims=True)
    powers = jnp.exp(scores - largest)
    weights = (powers / jnp.sum(powers, axis=-1, keepdims=True)).astype(jnp.bfloat16)
    values_heads = value_part.reshape(row_total, key_heads, head_width)
    mixed = jnp.einsum("kgpq,qkd->pkgd", weights, values_heads, preferred_element_type=jnp.float32)
    return mixed.astype(jnp.bfloat16).reshape(row_total, head_count * head_width)


def ring_pairs(rows, cols, step_row, step_col):
    return [
        (r * cols + c, ((r + step_row) % rows) * cols + (c + step_col) % cols)
        for r in range(rows)
        for c in range(cols)
    ]


def ring_gather(block, rows, cols, owners):
    expert_total = rows * cols
    up = lax.ppermute(block, "expert", ring_pairs(rows, cols, 1, 0))
    down = lax.ppermute(block, "expert", ring_pairs(rows, cols, -1, 0))
    up_two = lax.ppermute(up, "expert", ring_pairs(rows, cols, 1, 0))
    by_row = jnp.stack([block, down, up_two, up])
    walk = [
        (owner * expert_total + src, owner * expert_total + dst)
        for owner in range(owners)
        for src, dst in ring_pairs(rows, cols, 0, 1 if owner % 2 == 0 else -1)
    ]
    half = cols // 2
    mine = []
    current = by_row
    for step in range(half):
        current = lax.ppermute(current, ("dp", "expert"), walk)
        mine.append(current)
    mine = jnp.stack(mine)
    partner = lax.ppermute(mine[: half - 1], "dp", [(i, i ^ 1) for i in range(owners)])
    return jnp.concatenate([by_row[None], mine, partner], axis=0)


def project_heads(attended, output_weight):
    expert_total = lax.axis_size("expert")
    owner_total = lax.axis_size("dp")
    cols = 16
    rows = expert_total // cols
    if rows != 4 or expert_total % cols or owner_total % 2:
        return jnp.dot(
            attended,
            lax.all_gather(output_weight, "expert", axis=0, tiled=True),
            preferred_element_type=jnp.float32,
        )
    own = lax.axis_index("expert")
    own_row = own // cols
    own_col = own % cols
    sign = 1 - 2 * (lax.axis_index("dp") % 2)
    half = cols // 2
    steps = jnp.arange(1, half + 1, dtype=jnp.int32)
    offsets = jnp.concatenate(
        [jnp.zeros((1,), jnp.int32), -sign * steps, sign * steps[: half - 1]]
    )
    gathered = ring_gather(output_weight, rows, cols, owner_total)
    block = output_weight.shape[0]
    row_order = (own_row + jnp.arange(rows, dtype=jnp.int32)) % rows
    col_order = (own_col + offsets) % cols
    split = attended.reshape(attended.shape[0], rows, cols, block)
    split = jnp.take(jnp.take(split, col_order, axis=2), row_order, axis=1)
    split = jnp.swapaxes(split, 1, 2)
    return jnp.dot(
        split.reshape(attended.shape[0], -1),
        gathered.reshape(rows * cols * block, -1),
        preferred_element_type=jnp.float32,
    )


def hidden_product(block, gate_part, up_part, down_part):
    contract = (((1,), (1,)), ((), ()))
    gate_value = lax.dot_general(block, gate_part, contract, preferred_element_type=jnp.float32)
    up_value = lax.dot_general(block, up_part, contract, preferred_element_type=jnp.float32)
    active = (jax.nn.silu(gate_value) * up_value).astype(jnp.bfloat16)
    return jnp.dot(active, down_part, preferred_element_type=jnp.float32)


def expert_output(work_rows, gate_part, up_part, down_part):
    return hidden_product(work_rows, gate_part, up_part, down_part)


def local(
    query_rows,
    key_rows,
    value_rows,
    residual,
    document_owner,
    document_length,
    document_offset,
    query_gain,
    key_gain,
    output_weight,
    post_gain,
    routes,
    route_weight,
    gate_weight,
    up_weight,
    down_weight,
):
    owner_total = lax.axis_size("dp")
    expert_total = lax.axis_size("expert")
    row_total = query_rows.shape[0]
    capacity = row_total * 3 // (2 * owner_total)
    owners = document_owner[0]
    lengths = document_length[0]
    offsets = document_offset[0]
    starts = jnp.cumsum(lengths) - lengths
    owner_ids = jnp.arange(owner_total, dtype=jnp.int32)
    matches = owners[None, :] == owner_ids[:, None]
    start_of = jnp.sum(jnp.where(matches, starts[None, :], 0), axis=1)
    length_of = jnp.sum(jnp.where(matches, lengths[None, :], 0), axis=1)
    offset_of = jnp.sum(jnp.where(matches, offsets[None, :], 0), axis=1)
    slot_ids = jnp.arange(capacity, dtype=jnp.int32)
    source_rows = jnp.minimum(start_of[:, None] + slot_ids[None, :], row_total - 1).reshape(-1)
    pack_slot = jnp.where(
        slot_ids[None, :] < length_of[:, None], offset_of[:, None] + slot_ids[None, :], -1
    )
    total_slots = owner_total * capacity
    flat_slots = jnp.arange(total_slots, dtype=jnp.int32)
    pack_ids = jnp.arange(row_total, dtype=jnp.int32)
    whole_rows = jnp.concatenate([query_rows, key_rows, value_rows, residual], axis=1)
    widths = [query_rows.shape[1], key_rows.shape[1], value_rows.shape[1], residual.shape[1]]
    data_width = sum(widths)
    slot_column = jnp.broadcast_to(
        pack_slot.reshape(-1, 1).astype(jnp.bfloat16), (total_slots, 128)
    )
    outgoing_pack = jnp.concatenate([whole_rows[source_rows], slot_column], axis=1)
    got = lax.all_to_all(
        outgoing_pack.reshape(owner_total, capacity, -1),
        "dp",
        split_axis=0,
        concat_axis=0,
        tiled=True,
    ).reshape(total_slots, -1)
    got_slot = got[:, data_width].astype(jnp.int32)
    placed = got_slot[None, :] == pack_ids[:, None]
    slot_of = jnp.sum(jnp.where(placed, flat_slots[None, :], 0), axis=1)
    packed = got[slot_of]
    bounds = [0]
    for width in widths:
        bounds.append(bounds[-1] + width)
    pack_query, pack_key, pack_value, pack_residual = (
        packed[:, bounds[i] : bounds[i + 1]] for i in range(4)
    )
    identity = slot_of // capacity
    position = slot_of % capacity
    attended = attend(pack_query, pack_key, pack_value, identity, position, query_gain, key_gain)
    gate_whole, up_whole, down_whole = (
        lax.all_gather(gate_weight, "dp", axis=1, tiled=True),
        lax.all_gather(up_weight, "dp", axis=1, tiled=True),
        lax.all_gather(down_weight, "dp", axis=1, tiled=True),
    )
    attended, gate_whole, up_whole, down_whole = lax.optimization_barrier(
        (attended, gate_whole, up_whole, down_whole)
    )
    hidden_state = pack_residual.astype(jnp.float32) + project_heads(attended, output_weight)
    normed = rms_scale(hidden_state, post_gain).astype(jnp.bfloat16)
    top_total = routes.shape[1]
    most = row_total * top_total * 5 // (4 * expert_total)
    expert_ids = jnp.arange(expert_total, dtype=jnp.int32)
    routed = routes[:, :, None] == expert_ids[None, None, :]
    chosen = jnp.sum(routed.astype(jnp.int32), axis=1)
    earlier = (pack_ids[None, :] < pack_ids[:, None]).astype(jnp.int32)
    rank = jnp.dot(earlier, chosen)
    ranked = jnp.where(chosen > 0, rank, -1)
    place_ids = jnp.arange(most, dtype=jnp.int32)
    hits = ranked.T[:, :, None] == place_ids[None, None, :]
    source_token = jnp.sum(jnp.where(hits, pack_ids[None, :, None], 0), axis=1)
    picks = jnp.transpose(hits, (0, 2, 1)).reshape(-1, row_total).astype(jnp.bfloat16)
    outgoing = (
        jnp.dot(picks, normed, preferred_element_type=jnp.float32)
        .astype(jnp.bfloat16)
        .reshape(expert_total, most, -1)
    )
    total_rows = expert_total * most
    received = lax.all_to_all(outgoing, "expert", split_axis=0, concat_axis=0, tiled=True)
    work_rows = received.reshape(total_rows, -1)
    produced = expert_output(work_rows, gate_whole[0], up_whole[0], down_whole[0])
    produced = produced.astype(jnp.bfloat16)
    out_slots = produced.reshape(expert_total, most, -1)
    returned = lax.all_to_all(out_slots, "expert", split_axis=0, concat_axis=0, tiled=True)
    flat_back = returned.reshape(total_rows, -1)
    copy_rank = jnp.sum(jnp.where(routed, rank[:, None, :], 0), axis=2)
    copy_index = routes * most + copy_rank
    gates = route_weight / jnp.sum(route_weight, axis=1, keepdims=True)
    slot_ids_back = jnp.arange(total_rows, dtype=jnp.int32)
    spread = jnp.sum(
        jnp.where(copy_index[:, :, None] == slot_ids_back[None, None, :], gates[:, :, None], 0.0),
        axis=1,
    )
    mixture = jnp.zeros(hidden_state.shape, jnp.float32)
    for _ in range(3):
        leading = lax.reduce_precision(spread, exponent_bits=8, mantissa_bits=7)
        spread = spread - leading
        part = leading.astype(jnp.bfloat16)
        mixture = mixture + jnp.dot(part, flat_back, preferred_element_type=jnp.float32)
    return (hidden_state + mixture).astype(jnp.bfloat16)


def solution(mesh):
    placed = (
        P(("dp", "expert"), None),
        P(("dp", "expert"), None),
        P(("dp", "expert"), None),
        P(("dp", "expert"), None),
        P(("dp", "expert"), None),
        P(("dp", "expert"), None),
        P(("dp", "expert"), None),
        P(),
        P(),
        P("expert", None),
        P(),
        P(("dp", "expert"), None),
        P(("dp", "expert"), None),
        P("expert", "dp", None),
        P("expert", "dp", None),
        P("expert", "dp", None),
    )
    return jax.shard_map(
        local, mesh=mesh, in_specs=placed, out_specs=P(("dp", "expert"), None), check_vma=False
    )
```

```python
import jax
import jax.numpy as jnp
from jax import lax
from jax.sharding import PartitionSpec as P

norm_epsilon = 1e-06
rope_base = 1000000.0


def rms_scale(values, gain):
    mean_square = jnp.mean(values * values, axis=-1, keepdims=True)
    return values * lax.rsqrt(mean_square + norm_epsilon) * gain


def rotary(values, positions):
    head_width = values.shape[-1]
    half_width = head_width // 2
    frequency = rope_base ** (-2.0 * jnp.arange(half_width, dtype=jnp.float32) / head_width)
    angles = positions.astype(jnp.float32)[:, None] * frequency[None, :]
    cosine_part = jnp.cos(angles)[:, None, :]
    sine_part = jnp.sin(angles)[:, None, :]
    leading = values[..., :half_width]
    trailing = values[..., half_width:]
    return jnp.concatenate(
        [
            leading * cosine_part - trailing * sine_part,
            trailing * cosine_part + leading * sine_part,
        ],
        axis=-1,
    )


def attend(query_part, key_part, value_part, identity, position, query_gain, key_gain):
    row_total = query_part.shape[0]
    head_width = query_gain.shape[0]
    head_count = query_part.shape[1] // head_width
    key_heads = key_part.shape[1] // head_width
    group_size = head_count // key_heads
    queries = rotary(
        rms_scale(
            query_part.reshape(row_total, head_count, head_width).astype(jnp.float32), query_gain
        ),
        position,
    ).astype(jnp.bfloat16)
    keys_normed = rotary(
        rms_scale(key_part.reshape(row_total, key_heads, head_width).astype(jnp.float32), key_gain),
        position,
    ).astype(jnp.bfloat16)
    queries = queries.reshape(row_total, key_heads, group_size, head_width)
    scores = jnp.einsum(
        "pkgd,qkd->kgpq", queries, keys_normed, preferred_element_type=jnp.float32
    ) * head_width ** (-0.5)
    allowed = (identity[:, None] == identity[None, :]) & (position[None, :] <= position[:, None])
    scores = jnp.where(allowed, scores, -jnp.inf)
    largest = jnp.max(scores, axis=-1, keepdims=True)
    powers = jnp.exp(scores - largest)
    weights = (powers / jnp.sum(powers, axis=-1, keepdims=True)).astype(jnp.bfloat16)
    values_heads = value_part.reshape(row_total, key_heads, head_width)
    mixed = jnp.einsum("kgpq,qkd->pkgd", weights, values_heads, preferred_element_type=jnp.float32)
    return mixed.astype(jnp.bfloat16).reshape(row_total, head_count * head_width)


def ring_pairs(rows, cols, step_row, step_col):
    return [
        (r * cols + c, ((r + step_row) % rows) * cols + (c + step_col) % cols)
        for r in range(rows)
        for c in range(cols)
    ]


def ring_gather(block, rows, cols, owners):
    expert_total = rows * cols
    up = lax.ppermute(block, "expert", ring_pairs(rows, cols, 1, 0))
    down = lax.ppermute(block, "expert", ring_pairs(rows, cols, -1, 0))
    up_two = lax.ppermute(up, "expert", ring_pairs(rows, cols, 1, 0))
    by_row = jnp.stack([block, down, up_two, up])
    walk = [
        (owner * expert_total + src, owner * expert_total + dst)
        for owner in range(owners)
        for src, dst in ring_pairs(rows, cols, 0, 1 if owner % 2 == 0 else -1)
    ]
    half = cols // 2
    mine = []
    current = by_row
    for step in range(half):
        current = lax.ppermute(current, ("dp", "expert"), walk)
        mine.append(current)
    mine = jnp.stack(mine)
    partner = lax.ppermute(mine[: half - 1], "dp", [(i, i ^ 1) for i in range(owners)])
    return jnp.concatenate([by_row[None], mine, partner], axis=0)


def project_heads(attended, output_weight):
    expert_total = lax.axis_size("expert")
    owner_total = lax.axis_size("dp")
    cols = 16
    rows = expert_total // cols
    if rows != 4 or expert_total % cols or owner_total % 2:
        return jnp.dot(
            attended,
            lax.all_gather(output_weight, "expert", axis=0, tiled=True),
            preferred_element_type=jnp.float32,
        )
    own = lax.axis_index("expert")
    own_row = own // cols
    own_col = own % cols
    sign = 1 - 2 * (lax.axis_index("dp") % 2)
    half = cols // 2
    steps = jnp.arange(1, half + 1, dtype=jnp.int32)
    offsets = jnp.concatenate(
        [jnp.zeros((1,), jnp.int32), -sign * steps, sign * steps[: half - 1]]
    )
    gathered = ring_gather(output_weight, rows, cols, owner_total)
    block = output_weight.shape[0]
    row_order = (own_row + jnp.arange(rows, dtype=jnp.int32)) % rows
    col_order = (own_col + offsets) % cols
    split = attended.reshape(attended.shape[0], rows, cols, block)
    split = jnp.take(jnp.take(split, col_order, axis=2), row_order, axis=1)
    split = jnp.swapaxes(split, 1, 2)
    return jnp.dot(
        split.reshape(attended.shape[0], -1),
        gathered.reshape(rows * cols * block, -1),
        preferred_element_type=jnp.float32,
    )


def hidden_product(block, gate_part, up_part, down_part):
    contract = (((1,), (1,)), ((), ()))
    gate_value = lax.dot_general(block, gate_part, contract, preferred_element_type=jnp.float32)
    up_value = lax.dot_general(block, up_part, contract, preferred_element_type=jnp.float32)
    active = (jax.nn.silu(gate_value) * up_value).astype(jnp.bfloat16)
    return jnp.dot(active, down_part, preferred_element_type=jnp.float32)


def expert_output(work_rows, gate_part, up_part, down_part):
    return hidden_product(work_rows, gate_part, up_part, down_part)


def expert_exchange(slots):
    expert_total = lax.axis_size("expert")
    cols = 16
    rows = expert_total // cols
    if rows * cols != expert_total:
        return lax.all_to_all(slots, "expert", split_axis=0, concat_axis=0, tiled=True)
    grid = slots.reshape(rows, cols, *slots.shape[1:])
    along_row = [[r * cols + c for c in range(cols)] for r in range(rows)]
    along_col = [[r * cols + c for r in range(rows)] for c in range(cols)]
    grid = lax.all_to_all(
        grid, "expert", split_axis=1, concat_axis=1, tiled=True, axis_index_groups=along_row
    )
    grid = lax.all_to_all(
        grid, "expert", split_axis=0, concat_axis=0, tiled=True, axis_index_groups=along_col
    )
    return grid.reshape(slots.shape)


def local(
    query_rows,
    key_rows,
    value_rows,
    residual,
    document_owner,
    document_length,
    document_offset,
    query_gain,
    key_gain,
    output_weight,
    post_gain,
    routes,
    route_weight,
    gate_weight,
    up_weight,
    down_weight,
):
    owner_total = lax.axis_size("dp")
    expert_total = lax.axis_size("expert")
    row_total = query_rows.shape[0]
    capacity = row_total * 3 // (2 * owner_total)
    owners = document_owner[0]
    lengths = document_length[0]
    offsets = document_offset[0]
    starts = jnp.cumsum(lengths) - lengths
    owner_ids = jnp.arange(owner_total, dtype=jnp.int32)
    matches = owners[None, :] == owner_ids[:, None]
    start_of = jnp.sum(jnp.where(matches, starts[None, :], 0), axis=1)
    length_of = jnp.sum(jnp.where(matches, lengths[None, :], 0), axis=1)
    offset_of = jnp.sum(jnp.where(matches, offsets[None, :], 0), axis=1)
    slot_ids = jnp.arange(capacity, dtype=jnp.int32)
    source_rows = jnp.minimum(start_of[:, None] + slot_ids[None, :], row_total - 1).reshape(-1)
    pack_slot = jnp.where(
        slot_ids[None, :] < length_of[:, None], offset_of[:, None] + slot_ids[None, :], -1
    )
    total_slots = owner_total * capacity
    flat_slots = jnp.arange(total_slots, dtype=jnp.int32)
    pack_ids = jnp.arange(row_total, dtype=jnp.int32)
    whole_rows = jnp.concatenate([query_rows, key_rows, value_rows, residual], axis=1)
    widths = [query_rows.shape[1], key_rows.shape[1], value_rows.shape[1], residual.shape[1]]
    data_width = sum(widths)
    slot_column = jnp.broadcast_to(
        pack_slot.reshape(-1, 1).astype(jnp.bfloat16), (total_slots, 128)
    )
    outgoing_pack = jnp.concatenate([whole_rows[source_rows], slot_column], axis=1)
    got = lax.all_to_all(
        outgoing_pack.reshape(owner_total, capacity, -1),
        "dp",
        split_axis=0,
        concat_axis=0,
        tiled=True,
    ).reshape(total_slots, -1)
    got_slot = got[:, data_width].astype(jnp.int32)
    placed = got_slot[None, :] == pack_ids[:, None]
    slot_of = jnp.sum(jnp.where(placed, flat_slots[None, :], 0), axis=1)
    packed = got[slot_of]
    bounds = [0]
    for width in widths:
        bounds.append(bounds[-1] + width)
    pack_query, pack_key, pack_value, pack_residual = (
        packed[:, bounds[i] : bounds[i + 1]] for i in range(4)
    )
    identity = slot_of // capacity
    position = slot_of % capacity
    attended = attend(pack_query, pack_key, pack_value, identity, position, query_gain, key_gain)
    hidden_state = pack_residual.astype(jnp.float32) + project_heads(attended, output_weight)
    normed = rms_scale(hidden_state, post_gain).astype(jnp.bfloat16)
    top_total = routes.shape[1]
    most = row_total * top_total * 5 // (4 * expert_total)
    expert_ids = jnp.arange(expert_total, dtype=jnp.int32)
    routed = routes[:, :, None] == expert_ids[None, None, :]
    chosen = jnp.sum(routed.astype(jnp.int32), axis=1)
    earlier = (pack_ids[None, :] < pack_ids[:, None]).astype(jnp.int32)
    rank = jnp.dot(earlier, chosen)
    ranked = jnp.where(chosen > 0, rank, -1)
    place_ids = jnp.arange(most, dtype=jnp.int32)
    hits = ranked.T[:, :, None] == place_ids[None, None, :]
    source_token = jnp.sum(jnp.where(hits, pack_ids[None, :, None], 0), axis=1)
    picks = jnp.transpose(hits, (0, 2, 1)).reshape(-1, row_total).astype(jnp.bfloat16)
    outgoing = (
        jnp.dot(picks, normed, preferred_element_type=jnp.float32)
        .astype(jnp.bfloat16)
        .reshape(expert_total, most, -1)
    )
    total_rows = expert_total * most
    received = expert_exchange(outgoing)
    work_rows = received.reshape(total_rows, -1)
    gate_whole, up_whole, down_whole = (
        lax.all_gather(gate_weight, "dp", axis=1, tiled=True),
        lax.all_gather(up_weight, "dp", axis=1, tiled=True),
        lax.all_gather(down_weight, "dp", axis=1, tiled=True),
    )
    produced = expert_output(work_rows, gate_whole[0], up_whole[0], down_whole[0])
    produced = produced.astype(jnp.bfloat16)
    out_slots = produced.reshape(expert_total, most, -1)
    returned = expert_exchange(out_slots)
    flat_back = returned.reshape(total_rows, -1)
    copy_rank = jnp.sum(jnp.where(routed, rank[:, None, :], 0), axis=2)
    copy_index = routes * most + copy_rank
    gates = route_weight / jnp.sum(route_weight, axis=1, keepdims=True)
    slot_ids_back = jnp.arange(total_rows, dtype=jnp.int32)
    spread = jnp.sum(
        jnp.where(copy_index[:, :, None] == slot_ids_back[None, None, :], gates[:, :, None], 0.0),
        axis=1,
    )
    mixture = jnp.zeros(hidden_state.shape, jnp.float32)
    for _ in range(3):
        leading = lax.reduce_precision(spread, exponent_bits=8, mantissa_bits=7)
        spread = spread - leading
        part = leading.astype(jnp.bfloat16)
        mixture = mixture + jnp.dot(part, flat_back, preferred_element_type=jnp.float32)
    return (hidden_state + mixture).astype(jnp.bfloat16)


def solution(mesh):
    placed = (
        P(("dp", "expert"), None),
        P(("dp", "expert"), None),
        P(("dp", "expert"), None),
        P(("dp", "expert"), None),
        P(("dp", "expert"), None),
        P(("dp", "expert"), None),
        P(("dp", "expert"), None),
        P(),
        P(),
        P("expert", None),
        P(),
        P(("dp", "expert"), None),
        P(("dp", "expert"), None),
        P("expert", "dp", None),
        P("expert", "dp", None),
        P("expert", "dp", None),
    )
    return jax.shard_map(
        local, mesh=mesh, in_specs=placed, out_specs=P(("dp", "expert"), None), check_vma=False
    )
```

```python
import jax
import jax.numpy as jnp
from jax import lax
from jax.sharding import PartitionSpec as P

norm_epsilon = 1e-06
rope_base = 1000000.0


def rms_scale(values, gain):
    mean_square = jnp.mean(values * values, axis=-1, keepdims=True)
    return values * lax.rsqrt(mean_square + norm_epsilon) * gain


def rotary(values, positions):
    head_width = values.shape[-1]
    half_width = head_width // 2
    frequency = rope_base ** (-2.0 * jnp.arange(half_width, dtype=jnp.float32) / head_width)
    angles = positions.astype(jnp.float32)[:, None] * frequency[None, :]
    cosine_part = jnp.cos(angles)[:, None, :]
    sine_part = jnp.sin(angles)[:, None, :]
    leading = values[..., :half_width]
    trailing = values[..., half_width:]
    return jnp.concatenate(
        [
            leading * cosine_part - trailing * sine_part,
            trailing * cosine_part + leading * sine_part,
        ],
        axis=-1,
    )


def attend(query_part, key_part, value_part, identity, position, query_gain, key_gain):
    row_total = query_part.shape[0]
    head_width = query_gain.shape[0]
    head_count = query_part.shape[1] // head_width
    key_heads = key_part.shape[1] // head_width
    group_size = head_count // key_heads
    queries = rotary(
        rms_scale(
            query_part.reshape(row_total, head_count, head_width).astype(jnp.float32), query_gain
        ),
        position,
    ).astype(jnp.bfloat16)
    keys_normed = rotary(
        rms_scale(key_part.reshape(row_total, key_heads, head_width).astype(jnp.float32), key_gain),
        position,
    ).astype(jnp.bfloat16)
    queries = queries.reshape(row_total, key_heads, group_size, head_width)
    scores = jnp.einsum(
        "pkgd,qkd->kgpq", queries, keys_normed, preferred_element_type=jnp.float32
    ) * head_width ** (-0.5)
    allowed = (identity[:, None] == identity[None, :]) & (position[None, :] <= position[:, None])
    scores = jnp.where(allowed, scores, -jnp.inf)
    largest = jnp.max(scores, axis=-1, keepdims=True)
    powers = jnp.exp(scores - largest)
    weights = (powers / jnp.sum(powers, axis=-1, keepdims=True)).astype(jnp.bfloat16)
    values_heads = value_part.reshape(row_total, key_heads, head_width)
    mixed = jnp.einsum("kgpq,qkd->pkgd", weights, values_heads, preferred_element_type=jnp.float32)
    return mixed.astype(jnp.bfloat16).reshape(row_total, head_count * head_width)


def ring_pairs(rows, cols, step_row, step_col):
    return [
        (r * cols + c, ((r + step_row) % rows) * cols + (c + step_col) % cols)
        for r in range(rows)
        for c in range(cols)
    ]


def ring_gather(block, rows, cols, owners):
    expert_total = rows * cols
    up = lax.ppermute(block, "expert", ring_pairs(rows, cols, 1, 0))
    down = lax.ppermute(block, "expert", ring_pairs(rows, cols, -1, 0))
    up_two = lax.ppermute(up, "expert", ring_pairs(rows, cols, 1, 0))
    by_row = jnp.stack([block, down, up_two, up])
    walk = [
        (owner * expert_total + src, owner * expert_total + dst)
        for owner in range(owners)
        for src, dst in ring_pairs(rows, cols, 0, 1 if owner % 2 == 0 else -1)
    ]
    half = cols // 2
    mine = []
    current = by_row
    for step in range(half):
        current = lax.ppermute(current, ("dp", "expert"), walk)
        mine.append(current)
    mine = jnp.stack(mine)
    partner = lax.ppermute(mine[: half - 1], "dp", [(i, i ^ 1) for i in range(owners)])
    return by_row[None], mine, partner


def project_heads(attended, output_weight):
    expert_total = lax.axis_size("expert")
    owner_total = lax.axis_size("dp")
    cols = 16
    rows = expert_total // cols
    if rows != 4 or expert_total % cols or owner_total % 2:
        return jnp.dot(
            attended,
            lax.all_gather(output_weight, "expert", axis=0, tiled=True),
            preferred_element_type=jnp.float32,
        )
    own = lax.axis_index("expert")
    own_row = own // cols
    own_col = own % cols
    sign = 1 - 2 * (lax.axis_index("dp") % 2)
    half = cols // 2
    steps = jnp.arange(1, half + 1, dtype=jnp.int32)
    offsets = jnp.concatenate(
        [jnp.zeros((1,), jnp.int32), -sign * steps, sign * steps[: half - 1]]
    )
    gathered = ring_gather(output_weight, rows, cols, owner_total)
    block = output_weight.shape[0]
    row_order = (own_row + jnp.arange(rows, dtype=jnp.int32)) % rows
    col_order = (own_col + offsets) % cols
    split = attended.reshape(attended.shape[0], rows, cols, block)
    split = jnp.take(jnp.take(split, col_order, axis=2), row_order, axis=1)
    split = jnp.swapaxes(split, 1, 2)
    projected = jnp.zeros((attended.shape[0], output_weight.shape[1]), jnp.float32)
    first = 0
    for pieces in gathered:
        last = first + pieces.shape[0]
        projected = projected + jnp.dot(
            split[:, first:last].reshape(attended.shape[0], -1),
            pieces.reshape(-1, output_weight.shape[1]),
            preferred_element_type=jnp.float32,
        )
        first = last
    return projected


def hidden_product(block, gate_part, up_part, down_part):
    contract = (((1,), (1,)), ((), ()))
    gate_value = lax.dot_general(block, gate_part, contract, preferred_element_type=jnp.float32)
    up_value = lax.dot_general(block, up_part, contract, preferred_element_type=jnp.float32)
    active = (jax.nn.silu(gate_value) * up_value).astype(jnp.bfloat16)
    return jnp.dot(active, down_part, preferred_element_type=jnp.float32)


def expert_output(work_rows, gate_part, up_part, down_part):
    return hidden_product(work_rows, gate_part, up_part, down_part)


def local(
    query_rows,
    key_rows,
    value_rows,
    residual,
    document_owner,
    document_length,
    document_offset,
    query_gain,
    key_gain,
    output_weight,
    post_gain,
    routes,
    route_weight,
    gate_weight,
    up_weight,
    down_weight,
):
    owner_total = lax.axis_size("dp")
    expert_total = lax.axis_size("expert")
    row_total = query_rows.shape[0]
    capacity = row_total * 3 // (2 * owner_total)
    owners = document_owner[0]
    lengths = document_length[0]
    offsets = document_offset[0]
    starts = jnp.cumsum(lengths) - lengths
    owner_ids = jnp.arange(owner_total, dtype=jnp.int32)
    matches = owners[None, :] == owner_ids[:, None]
    start_of = jnp.sum(jnp.where(matches, starts[None, :], 0), axis=1)
    length_of = jnp.sum(jnp.where(matches, lengths[None, :], 0), axis=1)
    offset_of = jnp.sum(jnp.where(matches, offsets[None, :], 0), axis=1)
    slot_ids = jnp.arange(capacity, dtype=jnp.int32)
    source_rows = jnp.minimum(start_of[:, None] + slot_ids[None, :], row_total - 1).reshape(-1)
    pack_slot = jnp.where(
        slot_ids[None, :] < length_of[:, None], offset_of[:, None] + slot_ids[None, :], -1
    )
    total_slots = owner_total * capacity
    flat_slots = jnp.arange(total_slots, dtype=jnp.int32)
    pack_ids = jnp.arange(row_total, dtype=jnp.int32)
    whole_rows = jnp.concatenate([query_rows, key_rows, value_rows, residual], axis=1)
    widths = [query_rows.shape[1], key_rows.shape[1], value_rows.shape[1], residual.shape[1]]
    data_width = sum(widths)
    slot_column = jnp.broadcast_to(
        pack_slot.reshape(-1, 1).astype(jnp.bfloat16), (total_slots, 128)
    )
    outgoing_pack = jnp.concatenate([whole_rows[source_rows], slot_column], axis=1)
    got = lax.all_to_all(
        outgoing_pack.reshape(owner_total, capacity, -1),
        "dp",
        split_axis=0,
        concat_axis=0,
        tiled=True,
    ).reshape(total_slots, -1)
    got_slot = got[:, data_width].astype(jnp.int32)
    placed = got_slot[None, :] == pack_ids[:, None]
    slot_of = jnp.sum(jnp.where(placed, flat_slots[None, :], 0), axis=1)
    packed = got[slot_of]
    bounds = [0]
    for width in widths:
        bounds.append(bounds[-1] + width)
    pack_query, pack_key, pack_value, pack_residual = (
        packed[:, bounds[i] : bounds[i + 1]] for i in range(4)
    )
    identity = slot_of // capacity
    position = slot_of % capacity
    attended = attend(pack_query, pack_key, pack_value, identity, position, query_gain, key_gain)
    hidden_state = pack_residual.astype(jnp.float32) + project_heads(attended, output_weight)
    normed = rms_scale(hidden_state, post_gain).astype(jnp.bfloat16)
    top_total = routes.shape[1]
    most = row_total * top_total * 5 // (4 * expert_total)
    expert_ids = jnp.arange(expert_total, dtype=jnp.int32)
    routed = routes[:, :, None] == expert_ids[None, None, :]
    chosen = jnp.sum(routed.astype(jnp.int32), axis=1)
    earlier = (pack_ids[None, :] < pack_ids[:, None]).astype(jnp.int32)
    rank = jnp.dot(earlier, chosen)
    ranked = jnp.where(chosen > 0, rank, -1)
    place_ids = jnp.arange(most, dtype=jnp.int32)
    hits = ranked.T[:, :, None] == place_ids[None, None, :]
    source_token = jnp.sum(jnp.where(hits, pack_ids[None, :, None], 0), axis=1)
    picks = jnp.transpose(hits, (0, 2, 1)).reshape(-1, row_total).astype(jnp.bfloat16)
    outgoing = (
        jnp.dot(picks, normed, preferred_element_type=jnp.float32)
        .astype(jnp.bfloat16)
        .reshape(expert_total, most, -1)
    )
    total_rows = expert_total * most
    received = lax.all_to_all(outgoing, "expert", split_axis=0, concat_axis=0, tiled=True)
    work_rows = received.reshape(total_rows, -1)
    gate_whole, up_whole, down_whole = (
        lax.all_gather(gate_weight, "dp", axis=1, tiled=True),
        lax.all_gather(up_weight, "dp", axis=1, tiled=True),
        lax.all_gather(down_weight, "dp", axis=1, tiled=True),
    )
    produced = expert_output(work_rows, gate_whole[0], up_whole[0], down_whole[0])
    produced = produced.astype(jnp.bfloat16)
    out_slots = produced.reshape(expert_total, most, -1)
    returned = lax.all_to_all(out_slots, "expert", split_axis=0, concat_axis=0, tiled=True)
    flat_back = returned.reshape(total_rows, -1)
    copy_rank = jnp.sum(jnp.where(routed, rank[:, None, :], 0), axis=2)
    copy_index = routes * most + copy_rank
    gates = route_weight / jnp.sum(route_weight, axis=1, keepdims=True)
    slot_ids_back = jnp.arange(total_rows, dtype=jnp.int32)
    spread = jnp.sum(
        jnp.where(copy_index[:, :, None] == slot_ids_back[None, None, :], gates[:, :, None], 0.0),
        axis=1,
    )
    mixture = jnp.zeros(hidden_state.shape, jnp.float32)
    for _ in range(3):
        leading = lax.reduce_precision(spread, exponent_bits=8, mantissa_bits=7)
        spread = spread - leading
        part = leading.astype(jnp.bfloat16)
        mixture = mixture + jnp.dot(part, flat_back, preferred_element_type=jnp.float32)
    return (hidden_state + mixture).astype(jnp.bfloat16)


def solution(mesh):
    placed = (
        P(("dp", "expert"), None),
        P(("dp", "expert"), None),
        P(("dp", "expert"), None),
        P(("dp", "expert"), None),
        P(("dp", "expert"), None),
        P(("dp", "expert"), None),
        P(("dp", "expert"), None),
        P(),
        P(),
        P("expert", None),
        P(),
        P(("dp", "expert"), None),
        P(("dp", "expert"), None),
        P("expert", "dp", None),
        P("expert", "dp", None),
        P("expert", "dp", None),
    )
    return jax.shard_map(
        local, mesh=mesh, in_specs=placed, out_specs=P(("dp", "expert"), None), check_vma=False
    )
```

```python
import jax
import jax.numpy as jnp
from jax import lax
from jax.sharding import PartitionSpec as P

norm_epsilon = 1e-06
rope_base = 1000000.0


def rms_scale(values, gain):
    mean_square = jnp.mean(values * values, axis=-1, keepdims=True)
    return values * lax.rsqrt(mean_square + norm_epsilon) * gain


def rotary(values, positions):
    head_width = values.shape[-1]
    half_width = head_width // 2
    frequency = rope_base ** (-2.0 * jnp.arange(half_width, dtype=jnp.float32) / head_width)
    angles = positions.astype(jnp.float32)[:, None] * frequency[None, :]
    cosine_part = jnp.cos(angles)[:, None, :]
    sine_part = jnp.sin(angles)[:, None, :]
    leading = values[..., :half_width]
    trailing = values[..., half_width:]
    return jnp.concatenate(
        [
            leading * cosine_part - trailing * sine_part,
            trailing * cosine_part + leading * sine_part,
        ],
        axis=-1,
    )


def attend(query_part, key_part, value_part, identity, position, query_gain, key_gain):
    row_total = query_part.shape[0]
    head_width = query_gain.shape[0]
    head_count = query_part.shape[1] // head_width
    key_heads = key_part.shape[1] // head_width
    group_size = head_count // key_heads
    queries = rotary(
        rms_scale(
            query_part.reshape(row_total, head_count, head_width).astype(jnp.float32), query_gain
        ),
        position,
    ).astype(jnp.bfloat16)
    keys_normed = rotary(
        rms_scale(key_part.reshape(row_total, key_heads, head_width).astype(jnp.float32), key_gain),
        position,
    ).astype(jnp.bfloat16)
    queries = queries.reshape(row_total, key_heads, group_size, head_width)
    scores = jnp.einsum(
        "pkgd,qkd->kgpq", queries, keys_normed, preferred_element_type=jnp.float32
    ) * head_width ** (-0.5)
    allowed = (identity[:, None] == identity[None, :]) & (position[None, :] <= position[:, None])
    scores = jnp.where(allowed, scores, -jnp.inf)
    largest = jnp.max(scores, axis=-1, keepdims=True)
    powers = jnp.exp(scores - largest)
    weights = (powers / jnp.sum(powers, axis=-1, keepdims=True)).astype(jnp.bfloat16)
    values_heads = value_part.reshape(row_total, key_heads, head_width)
    mixed = jnp.einsum("kgpq,qkd->pkgd", weights, values_heads, preferred_element_type=jnp.float32)
    return mixed.astype(jnp.bfloat16).reshape(row_total, head_count * head_width)


def ring_pairs(rows, cols, step_row, step_col):
    return [
        (r * cols + c, ((r + step_row) % rows) * cols + (c + step_col) % cols)
        for r in range(rows)
        for c in range(cols)
    ]


def ring_gather(block, rows, cols, owners):
    expert_total = rows * cols
    up = lax.ppermute(block, "expert", ring_pairs(rows, cols, 1, 0))
    down = lax.ppermute(block, "expert", ring_pairs(rows, cols, -1, 0))
    up_two = lax.ppermute(up, "expert", ring_pairs(rows, cols, 1, 0))
    by_row = jnp.stack([block, down, up_two, up])
    def walk(stride):
        return [
            (owner * expert_total + src, owner * expert_total + dst)
            for owner in range(owners)
            for src, dst in ring_pairs(rows, cols, 0, stride if owner % 2 == 0 else -stride)
        ]

    half = cols // 2
    odd = lax.ppermute(by_row, ("dp", "expert"), walk(1))
    even = lax.ppermute(by_row, ("dp", "expert"), walk(2))
    mine = [odd, even]
    for _ in range(half // 2 - 1):
        odd = lax.ppermute(odd, ("dp", "expert"), walk(2))
        even = lax.ppermute(even, ("dp", "expert"), walk(2))
        mine += [odd, even]
    mine = jnp.stack(mine)
    partner = lax.ppermute(mine[: half - 1], "dp", [(i, i ^ 1) for i in range(owners)])
    return by_row[None], mine, partner


def project_heads(attended, output_weight):
    expert_total = lax.axis_size("expert")
    owner_total = lax.axis_size("dp")
    cols = 16
    rows = expert_total // cols
    if rows != 4 or expert_total % cols or owner_total % 2:
        return jnp.dot(
            attended,
            lax.all_gather(output_weight, "expert", axis=0, tiled=True),
            preferred_element_type=jnp.float32,
        )
    own = lax.axis_index("expert")
    own_row = own // cols
    own_col = own % cols
    sign = 1 - 2 * (lax.axis_index("dp") % 2)
    half = cols // 2
    steps = jnp.arange(1, half + 1, dtype=jnp.int32)
    offsets = jnp.concatenate(
        [jnp.zeros((1,), jnp.int32), -sign * steps, sign * steps[: half - 1]]
    )
    gathered = ring_gather(output_weight, rows, cols, owner_total)
    block = output_weight.shape[0]
    row_order = (own_row + jnp.arange(rows, dtype=jnp.int32)) % rows
    col_order = (own_col + offsets) % cols
    split = attended.reshape(attended.shape[0], rows, cols, block)
    split = jnp.take(jnp.take(split, col_order, axis=2), row_order, axis=1)
    split = jnp.swapaxes(split, 1, 2)
    projected = jnp.zeros((attended.shape[0], output_weight.shape[1]), jnp.float32)
    first = 0
    for pieces in gathered:
        last = first + pieces.shape[0]
        projected = projected + jnp.dot(
            split[:, first:last].reshape(attended.shape[0], -1),
            pieces.reshape(-1, output_weight.shape[1]),
            preferred_element_type=jnp.float32,
        )
        first = last
    return projected


def hidden_product(block, gate_part, up_part, down_part):
    contract = (((1,), (1,)), ((), ()))
    gate_value = lax.dot_general(block, gate_part, contract, preferred_element_type=jnp.float32)
    up_value = lax.dot_general(block, up_part, contract, preferred_element_type=jnp.float32)
    active = (jax.nn.silu(gate_value) * up_value).astype(jnp.bfloat16)
    return jnp.dot(active, down_part, preferred_element_type=jnp.float32)


def expert_output(work_rows, gate_part, up_part, down_part):
    return hidden_product(work_rows, gate_part, up_part, down_part)


def local(
    query_rows,
    key_rows,
    value_rows,
    residual,
    document_owner,
    document_length,
    document_offset,
    query_gain,
    key_gain,
    output_weight,
    post_gain,
    routes,
    route_weight,
    gate_weight,
    up_weight,
    down_weight,
):
    owner_total = lax.axis_size("dp")
    expert_total = lax.axis_size("expert")
    row_total = query_rows.shape[0]
    capacity = row_total * 3 // (2 * owner_total)
    owners = document_owner[0]
    lengths = document_length[0]
    offsets = document_offset[0]
    starts = jnp.cumsum(lengths) - lengths
    owner_ids = jnp.arange(owner_total, dtype=jnp.int32)
    matches = owners[None, :] == owner_ids[:, None]
    start_of = jnp.sum(jnp.where(matches, starts[None, :], 0), axis=1)
    length_of = jnp.sum(jnp.where(matches, lengths[None, :], 0), axis=1)
    offset_of = jnp.sum(jnp.where(matches, offsets[None, :], 0), axis=1)
    slot_ids = jnp.arange(capacity, dtype=jnp.int32)
    source_rows = jnp.minimum(start_of[:, None] + slot_ids[None, :], row_total - 1).reshape(-1)
    pack_slot = jnp.where(
        slot_ids[None, :] < length_of[:, None], offset_of[:, None] + slot_ids[None, :], -1
    )
    total_slots = owner_total * capacity
    flat_slots = jnp.arange(total_slots, dtype=jnp.int32)
    pack_ids = jnp.arange(row_total, dtype=jnp.int32)
    whole_rows = jnp.concatenate([query_rows, key_rows, value_rows, residual], axis=1)
    widths = [query_rows.shape[1], key_rows.shape[1], value_rows.shape[1], residual.shape[1]]
    data_width = sum(widths)
    slot_column = jnp.broadcast_to(
        pack_slot.reshape(-1, 1).astype(jnp.bfloat16), (total_slots, 128)
    )
    outgoing_pack = jnp.concatenate([whole_rows[source_rows], slot_column], axis=1)
    got = lax.all_to_all(
        outgoing_pack.reshape(owner_total, capacity, -1),
        "dp",
        split_axis=0,
        concat_axis=0,
        tiled=True,
    ).reshape(total_slots, -1)
    got_slot = got[:, data_width].astype(jnp.int32)
    placed = got_slot[None, :] == pack_ids[:, None]
    slot_of = jnp.sum(jnp.where(placed, flat_slots[None, :], 0), axis=1)
    packed = got[slot_of]
    bounds = [0]
    for width in widths:
        bounds.append(bounds[-1] + width)
    pack_query, pack_key, pack_value, pack_residual = (
        packed[:, bounds[i] : bounds[i + 1]] for i in range(4)
    )
    identity = slot_of // capacity
    position = slot_of % capacity
    attended = attend(pack_query, pack_key, pack_value, identity, position, query_gain, key_gain)
    hidden_state = pack_residual.astype(jnp.float32) + project_heads(attended, output_weight)
    normed = rms_scale(hidden_state, post_gain).astype(jnp.bfloat16)
    top_total = routes.shape[1]
    most = row_total * top_total * 5 // (4 * expert_total)
    expert_ids = jnp.arange(expert_total, dtype=jnp.int32)
    routed = routes[:, :, None] == expert_ids[None, None, :]
    chosen = jnp.sum(routed.astype(jnp.int32), axis=1)
    earlier = (pack_ids[None, :] < pack_ids[:, None]).astype(jnp.int32)
    rank = jnp.dot(earlier, chosen)
    ranked = jnp.where(chosen > 0, rank, -1)
    place_ids = jnp.arange(most, dtype=jnp.int32)
    hits = ranked.T[:, :, None] == place_ids[None, None, :]
    source_token = jnp.sum(jnp.where(hits, pack_ids[None, :, None], 0), axis=1)
    picks = jnp.transpose(hits, (0, 2, 1)).reshape(-1, row_total).astype(jnp.bfloat16)
    outgoing = (
        jnp.dot(picks, normed, preferred_element_type=jnp.float32)
        .astype(jnp.bfloat16)
        .reshape(expert_total, most, -1)
    )
    total_rows = expert_total * most
    received = lax.all_to_all(outgoing, "expert", split_axis=0, concat_axis=0, tiled=True)
    work_rows = received.reshape(total_rows, -1)
    gate_whole, up_whole, down_whole = (
        lax.all_gather(gate_weight, "dp", axis=1, tiled=True),
        lax.all_gather(up_weight, "dp", axis=1, tiled=True),
        lax.all_gather(down_weight, "dp", axis=1, tiled=True),
    )
    produced = expert_output(work_rows, gate_whole[0], up_whole[0], down_whole[0])
    produced = produced.astype(jnp.bfloat16)
    out_slots = produced.reshape(expert_total, most, -1)
    returned = lax.all_to_all(out_slots, "expert", split_axis=0, concat_axis=0, tiled=True)
    flat_back = returned.reshape(total_rows, -1)
    copy_rank = jnp.sum(jnp.where(routed, rank[:, None, :], 0), axis=2)
    copy_index = routes * most + copy_rank
    gates = route_weight / jnp.sum(route_weight, axis=1, keepdims=True)
    slot_ids_back = jnp.arange(total_rows, dtype=jnp.int32)
    spread = jnp.sum(
        jnp.where(copy_index[:, :, None] == slot_ids_back[None, None, :], gates[:, :, None], 0.0),
        axis=1,
    )
    mixture = jnp.zeros(hidden_state.shape, jnp.float32)
    for _ in range(3):
        leading = lax.reduce_precision(spread, exponent_bits=8, mantissa_bits=7)
        spread = spread - leading
        part = leading.astype(jnp.bfloat16)
        mixture = mixture + jnp.dot(part, flat_back, preferred_element_type=jnp.float32)
    return (hidden_state + mixture).astype(jnp.bfloat16)


def solution(mesh):
    placed = (
        P(("dp", "expert"), None),
        P(("dp", "expert"), None),
        P(("dp", "expert"), None),
        P(("dp", "expert"), None),
        P(("dp", "expert"), None),
        P(("dp", "expert"), None),
        P(("dp", "expert"), None),
        P(),
        P(),
        P("expert", None),
        P(),
        P(("dp", "expert"), None),
        P(("dp", "expert"), None),
        P("expert", "dp", None),
        P("expert", "dp", None),
        P("expert", "dp", None),
    )
    return jax.shard_map(
        local, mesh=mesh, in_specs=placed, out_specs=P(("dp", "expert"), None), check_vma=False
    )
```

```python
import jax
import jax.numpy as jnp
from jax import lax
from jax.sharding import PartitionSpec as P

norm_epsilon = 1e-06
rope_base = 1000000.0


def rms_scale(values, gain):
    mean_square = jnp.mean(values * values, axis=-1, keepdims=True)
    return values * lax.rsqrt(mean_square + norm_epsilon) * gain


def rotary(values, positions):
    head_width = values.shape[-1]
    half_width = head_width // 2
    frequency = rope_base ** (-2.0 * jnp.arange(half_width, dtype=jnp.float32) / head_width)
    angles = positions.astype(jnp.float32)[:, None] * frequency[None, :]
    cosine_part = jnp.cos(angles)[:, None, :]
    sine_part = jnp.sin(angles)[:, None, :]
    leading = values[..., :half_width]
    trailing = values[..., half_width:]
    return jnp.concatenate(
        [
            leading * cosine_part - trailing * sine_part,
            trailing * cosine_part + leading * sine_part,
        ],
        axis=-1,
    )


def attend(query_part, key_part, value_part, identity, position, query_gain, key_gain):
    row_total = query_part.shape[0]
    head_width = query_gain.shape[0]
    head_count = query_part.shape[1] // head_width
    key_heads = key_part.shape[1] // head_width
    group_size = head_count // key_heads
    queries = rotary(
        rms_scale(
            query_part.reshape(row_total, head_count, head_width).astype(jnp.float32), query_gain
        ),
        position,
    ).astype(jnp.bfloat16)
    keys_normed = rotary(
        rms_scale(key_part.reshape(row_total, key_heads, head_width).astype(jnp.float32), key_gain),
        position,
    ).astype(jnp.bfloat16)
    queries = queries.reshape(row_total, key_heads, group_size, head_width)
    scores = jnp.einsum(
        "pkgd,qkd->kgpq", queries, keys_normed, preferred_element_type=jnp.float32
    ) * head_width ** (-0.5)
    allowed = (identity[:, None] == identity[None, :]) & (position[None, :] <= position[:, None])
    scores = jnp.where(allowed, scores, -jnp.inf)
    largest = jnp.max(scores, axis=-1, keepdims=True)
    powers = jnp.exp(scores - largest)
    weights = (powers / jnp.sum(powers, axis=-1, keepdims=True)).astype(jnp.bfloat16)
    values_heads = value_part.reshape(row_total, key_heads, head_width)
    mixed = jnp.einsum("kgpq,qkd->pkgd", weights, values_heads, preferred_element_type=jnp.float32)
    return mixed.astype(jnp.bfloat16).reshape(row_total, head_count * head_width)


def ring_pairs(rows, cols, step_row, step_col):
    return [
        (r * cols + c, ((r + step_row) % rows) * cols + (c + step_col) % cols)
        for r in range(rows)
        for c in range(cols)
    ]


def ring_gather(block, rows, cols, owners):
    expert_total = rows * cols
    up = lax.ppermute(block, "expert", ring_pairs(rows, cols, 1, 0))
    down = lax.ppermute(block, "expert", ring_pairs(rows, cols, -1, 0))
    up_two = lax.ppermute(block, "expert", ring_pairs(rows, cols, 2, 0))
    by_row = jnp.stack([block, down, up_two, up])
    def walk(stride):
        return [
            (owner * expert_total + src, owner * expert_total + dst)
            for owner in range(owners)
            for src, dst in ring_pairs(rows, cols, 0, stride if owner % 2 == 0 else -stride)
        ]

    half = cols // 2
    odd = lax.ppermute(by_row, ("dp", "expert"), walk(1))
    even = lax.ppermute(by_row, ("dp", "expert"), walk(2))
    mine = [odd, even]
    for _ in range(half // 2 - 1):
        odd = lax.ppermute(odd, ("dp", "expert"), walk(2))
        even = lax.ppermute(even, ("dp", "expert"), walk(2))
        mine += [odd, even]
    mine = jnp.stack(mine)
    partner = lax.ppermute(mine[: half - 1], "dp", [(i, i ^ 1) for i in range(owners)])
    return by_row[None], mine, partner


def project_heads(attended, output_weight):
    expert_total = lax.axis_size("expert")
    owner_total = lax.axis_size("dp")
    cols = 16
    rows = expert_total // cols
    if rows != 4 or expert_total % cols or owner_total % 2:
        return jnp.dot(
            attended,
            lax.all_gather(output_weight, "expert", axis=0, tiled=True),
            preferred_element_type=jnp.float32,
        )
    own = lax.axis_index("expert")
    own_row = own // cols
    own_col = own % cols
    sign = 1 - 2 * (lax.axis_index("dp") % 2)
    half = cols // 2
    steps = jnp.arange(1, half + 1, dtype=jnp.int32)
    offsets = jnp.concatenate(
        [jnp.zeros((1,), jnp.int32), -sign * steps, sign * steps[: half - 1]]
    )
    gathered = ring_gather(output_weight, rows, cols, owner_total)
    block = output_weight.shape[0]
    row_order = (own_row + jnp.arange(rows, dtype=jnp.int32)) % rows
    col_order = (own_col + offsets) % cols
    split = attended.reshape(attended.shape[0], rows, cols, block)
    split = jnp.take(jnp.take(split, col_order, axis=2), row_order, axis=1)
    split = jnp.swapaxes(split, 1, 2)
    projected = jnp.zeros((attended.shape[0], output_weight.shape[1]), jnp.float32)
    first = 0
    for pieces in gathered:
        last = first + pieces.shape[0]
        projected = projected + jnp.dot(
            split[:, first:last].reshape(attended.shape[0], -1),
            pieces.reshape(-1, output_weight.shape[1]),
            preferred_element_type=jnp.float32,
        )
        first = last
    return projected


def hidden_product(block, gate_part, up_part, down_part):
    contract = (((1,), (1,)), ((), ()))
    gate_value = lax.dot_general(block, gate_part, contract, preferred_element_type=jnp.float32)
    up_value = lax.dot_general(block, up_part, contract, preferred_element_type=jnp.float32)
    active = (jax.nn.silu(gate_value) * up_value).astype(jnp.bfloat16)
    return jnp.dot(active, down_part, preferred_element_type=jnp.float32)


def expert_output(work_rows, gate_part, up_part, down_part):
    return hidden_product(work_rows, gate_part, up_part, down_part)


def local(
    query_rows,
    key_rows,
    value_rows,
    residual,
    document_owner,
    document_length,
    document_offset,
    query_gain,
    key_gain,
    output_weight,
    post_gain,
    routes,
    route_weight,
    gate_weight,
    up_weight,
    down_weight,
):
    owner_total = lax.axis_size("dp")
    expert_total = lax.axis_size("expert")
    row_total = query_rows.shape[0]
    capacity = row_total * 3 // (2 * owner_total)
    owners = document_owner[0]
    lengths = document_length[0]
    offsets = document_offset[0]
    starts = jnp.cumsum(lengths) - lengths
    owner_ids = jnp.arange(owner_total, dtype=jnp.int32)
    matches = owners[None, :] == owner_ids[:, None]
    start_of = jnp.sum(jnp.where(matches, starts[None, :], 0), axis=1)
    length_of = jnp.sum(jnp.where(matches, lengths[None, :], 0), axis=1)
    offset_of = jnp.sum(jnp.where(matches, offsets[None, :], 0), axis=1)
    slot_ids = jnp.arange(capacity, dtype=jnp.int32)
    source_rows = jnp.minimum(start_of[:, None] + slot_ids[None, :], row_total - 1).reshape(-1)
    pack_slot = jnp.where(
        slot_ids[None, :] < length_of[:, None], offset_of[:, None] + slot_ids[None, :], -1
    )
    total_slots = owner_total * capacity
    flat_slots = jnp.arange(total_slots, dtype=jnp.int32)
    pack_ids = jnp.arange(row_total, dtype=jnp.int32)
    whole_rows = jnp.concatenate([query_rows, key_rows, value_rows, residual], axis=1)
    widths = [query_rows.shape[1], key_rows.shape[1], value_rows.shape[1], residual.shape[1]]
    data_width = sum(widths)
    slot_column = jnp.broadcast_to(
        pack_slot.reshape(-1, 1).astype(jnp.bfloat16), (total_slots, 128)
    )
    outgoing_pack = jnp.concatenate([whole_rows[source_rows], slot_column], axis=1)
    got = lax.all_to_all(
        outgoing_pack.reshape(owner_total, capacity, -1),
        "dp",
        split_axis=0,
        concat_axis=0,
        tiled=True,
    ).reshape(total_slots, -1)
    got_slot = got[:, data_width].astype(jnp.int32)
    placed = got_slot[None, :] == pack_ids[:, None]
    slot_of = jnp.sum(jnp.where(placed, flat_slots[None, :], 0), axis=1)
    packed = got[slot_of]
    bounds = [0]
    for width in widths:
        bounds.append(bounds[-1] + width)
    pack_query, pack_key, pack_value, pack_residual = (
        packed[:, bounds[i] : bounds[i + 1]] for i in range(4)
    )
    identity = slot_of // capacity
    position = slot_of % capacity
    attended = attend(pack_query, pack_key, pack_value, identity, position, query_gain, key_gain)
    hidden_state = pack_residual.astype(jnp.float32) + project_heads(attended, output_weight)
    normed = rms_scale(hidden_state, post_gain).astype(jnp.bfloat16)
    top_total = routes.shape[1]
    most = row_total * top_total * 5 // (4 * expert_total)
    expert_ids = jnp.arange(expert_total, dtype=jnp.int32)
    routed = routes[:, :, None] == expert_ids[None, None, :]
    chosen = jnp.sum(routed.astype(jnp.int32), axis=1)
    earlier = (pack_ids[None, :] < pack_ids[:, None]).astype(jnp.int32)
    rank = jnp.dot(earlier, chosen)
    ranked = jnp.where(chosen > 0, rank, -1)
    place_ids = jnp.arange(most, dtype=jnp.int32)
    hits = ranked.T[:, :, None] == place_ids[None, None, :]
    source_token = jnp.sum(jnp.where(hits, pack_ids[None, :, None], 0), axis=1)
    picks = jnp.transpose(hits, (0, 2, 1)).reshape(-1, row_total).astype(jnp.bfloat16)
    outgoing = (
        jnp.dot(picks, normed, preferred_element_type=jnp.float32)
        .astype(jnp.bfloat16)
        .reshape(expert_total, most, -1)
    )
    total_rows = expert_total * most
    received = lax.all_to_all(outgoing, "expert", split_axis=0, concat_axis=0, tiled=True)
    work_rows = received.reshape(total_rows, -1)
    gate_whole, up_whole, down_whole = (
        lax.all_gather(gate_weight, "dp", axis=1, tiled=True),
        lax.all_gather(up_weight, "dp", axis=1, tiled=True),
        lax.all_gather(down_weight, "dp", axis=1, tiled=True),
    )
    produced = expert_output(work_rows, gate_whole[0], up_whole[0], down_whole[0])
    produced = produced.astype(jnp.bfloat16)
    out_slots = produced.reshape(expert_total, most, -1)
    returned = lax.all_to_all(out_slots, "expert", split_axis=0, concat_axis=0, tiled=True)
    flat_back = returned.reshape(total_rows, -1)
    copy_rank = jnp.sum(jnp.where(routed, rank[:, None, :], 0), axis=2)
    copy_index = routes * most + copy_rank
    gates = route_weight / jnp.sum(route_weight, axis=1, keepdims=True)
    slot_ids_back = jnp.arange(total_rows, dtype=jnp.int32)
    spread = jnp.sum(
        jnp.where(copy_index[:, :, None] == slot_ids_back[None, None, :], gates[:, :, None], 0.0),
        axis=1,
    )
    mixture = jnp.zeros(hidden_state.shape, jnp.float32)
    for _ in range(3):
        leading = lax.reduce_precision(spread, exponent_bits=8, mantissa_bits=7)
        spread = spread - leading
        part = leading.astype(jnp.bfloat16)
        mixture = mixture + jnp.dot(part, flat_back, preferred_element_type=jnp.float32)
    return (hidden_state + mixture).astype(jnp.bfloat16)


def solution(mesh):
    placed = (
        P(("dp", "expert"), None),
        P(("dp", "expert"), None),
        P(("dp", "expert"), None),
        P(("dp", "expert"), None),
        P(("dp", "expert"), None),
        P(("dp", "expert"), None),
        P(("dp", "expert"), None),
        P(),
        P(),
        P("expert", None),
        P(),
        P(("dp", "expert"), None),
        P(("dp", "expert"), None),
        P("expert", "dp", None),
        P("expert", "dp", None),
        P("expert", "dp", None),
    )
    return jax.shard_map(
        local, mesh=mesh, in_specs=placed, out_specs=P(("dp", "expert"), None), check_vma=False
    )
```

```python
import jax
import jax.numpy as jnp
from jax import lax
from jax.sharding import PartitionSpec as P

norm_epsilon = 1e-06
rope_base = 1000000.0


def rms_scale(values, gain):
    mean_square = jnp.mean(values * values, axis=-1, keepdims=True)
    return values * lax.rsqrt(mean_square + norm_epsilon) * gain


def rotary(values, positions):
    head_width = values.shape[-1]
    half_width = head_width // 2
    frequency = rope_base ** (-2.0 * jnp.arange(half_width, dtype=jnp.float32) / head_width)
    angles = positions.astype(jnp.float32)[:, None] * frequency[None, :]
    cosine_part = jnp.cos(angles)[:, None, :]
    sine_part = jnp.sin(angles)[:, None, :]
    leading = values[..., :half_width]
    trailing = values[..., half_width:]
    return jnp.concatenate(
        [
            leading * cosine_part - trailing * sine_part,
            trailing * cosine_part + leading * sine_part,
        ],
        axis=-1,
    )


def attend(query_part, key_part, value_part, identity, position, query_gain, key_gain):
    row_total = query_part.shape[0]
    head_width = query_gain.shape[0]
    head_count = query_part.shape[1] // head_width
    key_heads = key_part.shape[1] // head_width
    group_size = head_count // key_heads
    queries = rotary(
        rms_scale(
            query_part.reshape(row_total, head_count, head_width).astype(jnp.float32), query_gain
        ),
        position,
    ).astype(jnp.bfloat16)
    keys_normed = rotary(
        rms_scale(key_part.reshape(row_total, key_heads, head_width).astype(jnp.float32), key_gain),
        position,
    ).astype(jnp.bfloat16)
    queries = queries.reshape(row_total, key_heads, group_size, head_width)
    scores = jnp.einsum(
        "pkgd,qkd->kgpq", queries, keys_normed, preferred_element_type=jnp.float32
    ) * head_width ** (-0.5)
    allowed = (identity[:, None] == identity[None, :]) & (position[None, :] <= position[:, None])
    scores = jnp.where(allowed, scores, -jnp.inf)
    largest = jnp.max(scores, axis=-1, keepdims=True)
    powers = jnp.exp(scores - largest)
    weights = (powers / jnp.sum(powers, axis=-1, keepdims=True)).astype(jnp.bfloat16)
    values_heads = value_part.reshape(row_total, key_heads, head_width)
    mixed = jnp.einsum("kgpq,qkd->pkgd", weights, values_heads, preferred_element_type=jnp.float32)
    return mixed.astype(jnp.bfloat16).reshape(row_total, head_count * head_width)


def ring_pairs(rows, cols, step_row, step_col):
    return [
        (r * cols + c, ((r + step_row) % rows) * cols + (c + step_col) % cols)
        for r in range(rows)
        for c in range(cols)
    ]


def ring_gather(block, rows, cols, owners):
    expert_total = rows * cols
    up = lax.ppermute(block, "expert", ring_pairs(rows, cols, 1, 0))
    down = lax.ppermute(block, "expert", ring_pairs(rows, cols, -1, 0))
    up_two = lax.ppermute(block, "expert", ring_pairs(rows, cols, 2, 0))
    by_row = jnp.stack([block, down, up_two, up])
    def walk(stride):
        return [
            (owner * expert_total + src, owner * expert_total + dst)
            for owner in range(owners)
            for src, dst in ring_pairs(rows, cols, 0, stride if owner % 2 == 0 else -stride)
        ]

    half = cols // 2
    stride = 3
    chains = [lax.ppermute(by_row, ("dp", "expert"), walk(s)) for s in range(1, stride + 1)]
    found = {s: chains[s - 1] for s in range(1, stride + 1)}
    reach = stride
    while reach < half:
        chains = [
            lax.ppermute(chain, ("dp", "expert"), walk(stride))
            for s, chain in enumerate(chains, start=reach + 1)
            if s <= half
        ]
        for s, chain in enumerate(chains, start=reach + 1):
            found[s] = chain
        reach += stride
    mine = [found[s] for s in range(1, half + 1)]
    mine = jnp.stack(mine)
    partner = lax.ppermute(mine[: half - 1], "dp", [(i, i ^ 1) for i in range(owners)])
    return by_row[None], mine, partner


def project_heads(attended, output_weight):
    expert_total = lax.axis_size("expert")
    owner_total = lax.axis_size("dp")
    cols = 16
    rows = expert_total // cols
    if rows != 4 or expert_total % cols or owner_total % 2:
        return jnp.dot(
            attended,
            lax.all_gather(output_weight, "expert", axis=0, tiled=True),
            preferred_element_type=jnp.float32,
        )
    own = lax.axis_index("expert")
    own_row = own // cols
    own_col = own % cols
    sign = 1 - 2 * (lax.axis_index("dp") % 2)
    half = cols // 2
    steps = jnp.arange(1, half + 1, dtype=jnp.int32)
    offsets = jnp.concatenate(
        [jnp.zeros((1,), jnp.int32), -sign * steps, sign * steps[: half - 1]]
    )
    gathered = ring_gather(output_weight, rows, cols, owner_total)
    block = output_weight.shape[0]
    row_order = (own_row + jnp.arange(rows, dtype=jnp.int32)) % rows
    col_order = (own_col + offsets) % cols
    split = attended.reshape(attended.shape[0], rows, cols, block)
    split = jnp.take(jnp.take(split, col_order, axis=2), row_order, axis=1)
    split = jnp.swapaxes(split, 1, 2)
    projected = jnp.zeros((attended.shape[0], output_weight.shape[1]), jnp.float32)
    first = 0
    for pieces in gathered:
        last = first + pieces.shape[0]
        projected = projected + jnp.dot(
            split[:, first:last].reshape(attended.shape[0], -1),
            pieces.reshape(-1, output_weight.shape[1]),
            preferred_element_type=jnp.float32,
        )
        first = last
    return projected


def hidden_product(block, gate_part, up_part, down_part):
    contract = (((1,), (1,)), ((), ()))
    gate_value = lax.dot_general(block, gate_part, contract, preferred_element_type=jnp.float32)
    up_value = lax.dot_general(block, up_part, contract, preferred_element_type=jnp.float32)
    active = (jax.nn.silu(gate_value) * up_value).astype(jnp.bfloat16)
    return jnp.dot(active, down_part, preferred_element_type=jnp.float32)


def expert_output(work_rows, gate_part, up_part, down_part):
    return hidden_product(work_rows, gate_part, up_part, down_part)


def local(
    query_rows,
    key_rows,
    value_rows,
    residual,
    document_owner,
    document_length,
    document_offset,
    query_gain,
    key_gain,
    output_weight,
    post_gain,
    routes,
    route_weight,
    gate_weight,
    up_weight,
    down_weight,
):
    owner_total = lax.axis_size("dp")
    expert_total = lax.axis_size("expert")
    row_total = query_rows.shape[0]
    capacity = row_total * 3 // (2 * owner_total)
    owners = document_owner[0]
    lengths = document_length[0]
    offsets = document_offset[0]
    starts = jnp.cumsum(lengths) - lengths
    owner_ids = jnp.arange(owner_total, dtype=jnp.int32)
    matches = owners[None, :] == owner_ids[:, None]
    start_of = jnp.sum(jnp.where(matches, starts[None, :], 0), axis=1)
    length_of = jnp.sum(jnp.where(matches, lengths[None, :], 0), axis=1)
    offset_of = jnp.sum(jnp.where(matches, offsets[None, :], 0), axis=1)
    slot_ids = jnp.arange(capacity, dtype=jnp.int32)
    source_rows = jnp.minimum(start_of[:, None] + slot_ids[None, :], row_total - 1).reshape(-1)
    pack_slot = jnp.where(
        slot_ids[None, :] < length_of[:, None], offset_of[:, None] + slot_ids[None, :], -1
    )
    total_slots = owner_total * capacity
    flat_slots = jnp.arange(total_slots, dtype=jnp.int32)
    pack_ids = jnp.arange(row_total, dtype=jnp.int32)
    whole_rows = jnp.concatenate([query_rows, key_rows, value_rows, residual], axis=1)
    widths = [query_rows.shape[1], key_rows.shape[1], value_rows.shape[1], residual.shape[1]]
    data_width = sum(widths)
    slot_column = jnp.broadcast_to(
        pack_slot.reshape(-1, 1).astype(jnp.bfloat16), (total_slots, 128)
    )
    outgoing_pack = jnp.concatenate([whole_rows[source_rows], slot_column], axis=1)
    got = lax.all_to_all(
        outgoing_pack.reshape(owner_total, capacity, -1),
        "dp",
        split_axis=0,
        concat_axis=0,
        tiled=True,
    ).reshape(total_slots, -1)
    got_slot = got[:, data_width].astype(jnp.int32)
    placed = got_slot[None, :] == pack_ids[:, None]
    slot_of = jnp.sum(jnp.where(placed, flat_slots[None, :], 0), axis=1)
    packed = got[slot_of]
    bounds = [0]
    for width in widths:
        bounds.append(bounds[-1] + width)
    pack_query, pack_key, pack_value, pack_residual = (
        packed[:, bounds[i] : bounds[i + 1]] for i in range(4)
    )
    identity = slot_of // capacity
    position = slot_of % capacity
    attended = attend(pack_query, pack_key, pack_value, identity, position, query_gain, key_gain)
    hidden_state = pack_residual.astype(jnp.float32) + project_heads(attended, output_weight)
    normed = rms_scale(hidden_state, post_gain).astype(jnp.bfloat16)
    top_total = routes.shape[1]
    most = row_total * top_total * 5 // (4 * expert_total)
    expert_ids = jnp.arange(expert_total, dtype=jnp.int32)
    routed = routes[:, :, None] == expert_ids[None, None, :]
    chosen = jnp.sum(routed.astype(jnp.int32), axis=1)
    earlier = (pack_ids[None, :] < pack_ids[:, None]).astype(jnp.int32)
    rank = jnp.dot(earlier, chosen)
    ranked = jnp.where(chosen > 0, rank, -1)
    place_ids = jnp.arange(most, dtype=jnp.int32)
    hits = ranked.T[:, :, None] == place_ids[None, None, :]
    source_token = jnp.sum(jnp.where(hits, pack_ids[None, :, None], 0), axis=1)
    picks = jnp.transpose(hits, (0, 2, 1)).reshape(-1, row_total).astype(jnp.bfloat16)
    outgoing = (
        jnp.dot(picks, normed, preferred_element_type=jnp.float32)
        .astype(jnp.bfloat16)
        .reshape(expert_total, most, -1)
    )
    total_rows = expert_total * most
    received = lax.all_to_all(outgoing, "expert", split_axis=0, concat_axis=0, tiled=True)
    work_rows = received.reshape(total_rows, -1)
    gate_whole, up_whole, down_whole = (
        lax.all_gather(gate_weight, "dp", axis=1, tiled=True),
        lax.all_gather(up_weight, "dp", axis=1, tiled=True),
        lax.all_gather(down_weight, "dp", axis=1, tiled=True),
    )
    produced = expert_output(work_rows, gate_whole[0], up_whole[0], down_whole[0])
    produced = produced.astype(jnp.bfloat16)
    out_slots = produced.reshape(expert_total, most, -1)
    returned = lax.all_to_all(out_slots, "expert", split_axis=0, concat_axis=0, tiled=True)
    flat_back = returned.reshape(total_rows, -1)
    copy_rank = jnp.sum(jnp.where(routed, rank[:, None, :], 0), axis=2)
    copy_index = routes * most + copy_rank
    gates = route_weight / jnp.sum(route_weight, axis=1, keepdims=True)
    slot_ids_back = jnp.arange(total_rows, dtype=jnp.int32)
    spread = jnp.sum(
        jnp.where(copy_index[:, :, None] == slot_ids_back[None, None, :], gates[:, :, None], 0.0),
        axis=1,
    )
    mixture = jnp.zeros(hidden_state.shape, jnp.float32)
    for _ in range(3):
        leading = lax.reduce_precision(spread, exponent_bits=8, mantissa_bits=7)
        spread = spread - leading
        part = leading.astype(jnp.bfloat16)
        mixture = mixture + jnp.dot(part, flat_back, preferred_element_type=jnp.float32)
    return (hidden_state + mixture).astype(jnp.bfloat16)


def solution(mesh):
    placed = (
        P(("dp", "expert"), None),
        P(("dp", "expert"), None),
        P(("dp", "expert"), None),
        P(("dp", "expert"), None),
        P(("dp", "expert"), None),
        P(("dp", "expert"), None),
        P(("dp", "expert"), None),
        P(),
        P(),
        P("expert", None),
        P(),
        P(("dp", "expert"), None),
        P(("dp", "expert"), None),
        P("expert", "dp", None),
        P("expert", "dp", None),
        P("expert", "dp", None),
    )
    return jax.shard_map(
        local, mesh=mesh, in_specs=placed, out_specs=P(("dp", "expert"), None), check_vma=False
    )
```
